128 devices in a mesh: task: 4 (over x), ex: 32 (over z, y, core).
Axes of the slice: x: 4, y: 4, z: 4, core: 2. Of those that a mesh axis runs over, the one named last changes fastest.
Arguments:
- feats: bfloat16 [1536, 8, 8, 512], P(('task', 'ex')), may hold values from -25 to 25
- targets: int32 [1536, 64], P(('task', 'ex')), may hold values from 0 to 9
- task_of: int32 [1536], P(('task', 'ex')), may hold values from 0 to 3, as said below
- counts: int32 [4], P('task'), may hold values from 192 to 576, as said below
- down_w: float32 [4, 3, 3, 512, 256], P('task'), may hold values from -0.09375 to 0.09375
- up_w: float32 [4, 256, 512], P('task'), may hold values from -0.375 to 0.375
- head: bfloat16 [512, 10], replicated, may hold values from -0.14941406 to 0.14941406
Outputs:
- down_new: float32 [4, 3, 3, 512, 256], P('task', None, None, 'ex')
- up_new: float32 [4, 256, 512], P('task', 'ex')
- losses: float32 [4, 2], P('task')
The draws below stay inside these ranges and needn't reach their ends.
Inputs may be any that keep to these rules, and one draw needn't show every extreme that they name: The 12 rows of each device's block of task_of are the examples augmented on that device; each example is trained in the group of its task on the device with the same ex index as the device that holds it. The rows of one device name one task at most 6 times, and some device does so; the devices of one ex index hold together at most 24 examples of one task, and some task reaches that. counts[g] is the number of rows of task_of equal to g; both bounds are reached.
All inputs are finite; a program needn't handle non-finite values.
Results may differ from the reference program's by a relative error of at most 0.002.
Values may be sent and summed in bfloat16 or wider, within the bound.
No kernel may reach another device: no remote copies, remote signals or barrier semaphores. Data moves between devices by JAX's collectives and lax.ppermute only.
A program may use at most 128 MiB of HBM per device.

```python
import math
import jax
import jax.numpy as jnp
from jax import lax

CHANNELS = 512
INNER = 256
COLOURS = 10
GRID_SIDE = 8
TRAIN_STEPS = 2
EXAMPLES_DEV = 12
GRID_CELLS = 64
ALL_TASKS = 4
EXAMPLES = 1536
GROUP_MOST = 576
N_TASK = 4
N_EX = 32


def route_plan(key):
    pair_count = N_TASK // 2
    column_pairs = N_EX // 2
    halfway = EXAMPLES_DEV // 2
    order = jax.random.permutation(jax.random.fold_in(key, 1), N_TASK)
    shifts = jax.random.randint(jax.random.fold_in(key, 2), (pair_count,), 0, halfway + 1, dtype=jnp.int32)
    shifts = shifts.at[0].set(halfway)
    columns = jax.random.permutation(jax.random.fold_in(key, 3), N_EX)
    swings = jax.random.randint(jax.random.fold_in(key, 4), (pair_count, column_pairs), 0, halfway + 1, dtype=jnp.int32)
    swings = swings.at[0, 0].set(halfway)
    placed = jnp.stack([swings, -swings], axis=2).reshape(pair_count, N_EX)
    spread = jnp.zeros((pair_count, N_EX), jnp.int32).at[:, columns].set(placed)
    first = EXAMPLES_DEV + shifts[:, None] + spread
    second = 2 * EXAMPLES_DEV - first
    demand = jnp.zeros((N_TASK, N_EX), jnp.int32).at[order[0::2]].set(first).at[order[1::2]].set(second)
    totals = jnp.sum(demand, axis=1)
    run_keys = jax.random.split(jax.random.fold_in(key, 5), N_EX)
    runs = jax.vmap(lambda single: jax.random.permutation(single, N_TASK))(run_keys)
    lengths = jnp.take_along_axis(demand.T, runs, axis=1)
    finish = jnp.cumsum(lengths, axis=1)
    places = jnp.arange(N_TASK * EXAMPLES_DEV, dtype=jnp.int32)
    within = jnp.sum((places[None, :, None] >= finish[:, None, :]).astype(jnp.int32), axis=2)
    chosen = jnp.take_along_axis(runs, within, axis=1)
    chosen = chosen.reshape(N_EX, EXAMPLES_DEV, N_TASK)
    owners = jnp.transpose(chosen, (2, 0, 1)).reshape(N_TASK * N_EX * EXAMPLES_DEV)
    return (owners.astype(jnp.int32), totals.astype(jnp.int32))


def draw_task_of(key, part):
    owners, totals = route_plan(key)
    return owners


def draw_counts(key, part):
    owners, totals = route_plan(key)
    return totals


def draw_feats(key, part):
    shape = (EXAMPLES, GRID_SIDE, GRID_SIDE, CHANNELS)
    channel_scale = jnp.exp(jax.random.uniform(jax.random.fold_in(key, 21), (CHANNELS,), jnp.float32, math.log(0.3), math.log(3.0)))
    values = jnp.clip(jax.random.normal(jax.random.fold_in(key, 22), shape, jnp.float32), -6.0, 6.0)
    return (values * channel_scale).astype(jnp.bfloat16)


def place_ends(drawn, key, smallest, top_value):
    spot = [jax.random.randint(jax.random.fold_in(key, axis), (), 0, length) for axis, length in enumerate(drawn.shape)]
    main_axis = drawn.shape.index(max(drawn.shape))
    beside = spot[:main_axis] + [(spot[main_axis] + 1) % drawn.shape[main_axis]] + spot[main_axis + 1:]
    return drawn.at[tuple(spot)].set(smallest).at[tuple(beside)].set(top_value)


def steps_of(stream_key, shape, cuts, low, high):
    loudness, own = 1.0, jax.random.fold_in(stream_key, 6)
    for position, parts in cuts:
        steps = jnp.exp(jax.random.uniform(jax.random.fold_in(own, position), (parts,), jnp.float32, low / len(cuts), high / len(cuts)))
        loudness = loudness * jnp.repeat(steps, shape[position] // parts).reshape([-1 if axis == position else 1 for axis in range(len(shape))])
    return loudness


def normal_values(own_key, extent, scale, most, shards=(), kind=jnp.bfloat16):
    factor_of = steps_of(own_key, extent, shards, -0.22, 0.18) if shards else 1.0
    result = jax.random.normal(own_key, extent, jnp.float32) * scale * factor_of
    return jnp.minimum(jnp.maximum(result, -most), most).astype(kind)


def setup_inputs(seed: int = 0) -> dict:
    key_list = jax.random.split(jax.random.key(seed), 8)
    return {
        "feats": draw_feats(jax.random.fold_in(key_list[7], 71), 0),
        "targets": place_ends(jax.random.randint(key_list[1], (EXAMPLES, GRID_CELLS), 0, COLOURS), jax.random.fold_in(key_list[1], 1), 0, COLOURS - 1).astype(jnp.int32),
        "task_of": draw_task_of(jax.random.fold_in(key_list[7], 71), 0),
        "counts": draw_counts(jax.random.fold_in(key_list[7], 71), 0),
        "down_w": normal_values(key_list[4], (ALL_TASKS, 3, 3, CHANNELS, INNER), (9 * CHANNELS) ** -0.5, 0.09375, ((0, 4),), jnp.float32),
        "up_w": normal_values(key_list[5], (ALL_TASKS, INNER, CHANNELS), INNER ** -0.5, 0.375, ((0, 4),), jnp.float32),
        "head": jnp.clip(jax.random.uniform(key_list[6], (CHANNELS, COLOURS), jnp.float32, -0.14941406, 0.14941406), -0.14941406, 0.14941406).astype(jnp.bfloat16),
    }


def shifted_windows(grids):
    count_rows = grids.shape[0]
    side = grids.shape[1]
    padded = jnp.pad(grids, ((0, 0), (1, 1), (1, 1), (0, 0)))
    windows = []
    for offset_index in range(9):
        row_shift = offset_index // 3
        col_shift = offset_index % 3
        window = padded[:, row_shift:row_shift + side, col_shift:col_shift + side, :]
        windows.append(window.reshape(count_rows * side * side, grids.shape[3]))
    return windows

def contract_rows(left, right):
    return lax.dot_general(left, right, (((0,), (0,)), ((), ())), preferred_element_type=jnp.float32)

def train_pass(grids, labels, down_low, up_low, head, count):
    windows = shifted_windows(grids)
    flat_rows = windows[0].shape[0]
    middle = jnp.zeros((flat_rows, down_low.shape[3]), jnp.float32)
    for offset_index in range(9):
        middle = middle + jnp.dot(windows[offset_index], down_low[offset_index // 3, offset_index % 3], preferred_element_type=jnp.float32)
    active = jax.nn.silu(middle).astype(jnp.bfloat16)
    hidden = grids.reshape(flat_rows, grids.shape[3]).astype(jnp.float32) + jnp.dot(active, up_low, preferred_element_type=jnp.float32)
    inverse = lax.rsqrt(lax.optimization_barrier(jnp.mean(hidden * hidden, axis=-1, keepdims=True)) + 1e-06)
    normed = hidden * inverse
    head_wide = head.astype(jnp.float32)
    logits = jnp.dot(normed, head_wide, precision=lax.Precision.HIGHEST, preferred_element_type=jnp.float32)
    flat_labels = labels.reshape(flat_rows)
    living = (flat_labels >= 0).astype(jnp.float32)
    onehot = (flat_labels[:, None] == jnp.arange(head.shape[1], dtype=jnp.int32)[None, :]).astype(jnp.float32)
    powers = jnp.exp(logits)
    totals = lax.optimization_barrier(jnp.sum(powers, axis=-1))
    loss_sum = jnp.sum((jnp.log(totals) - lax.optimization_barrier(jnp.sum(logits * onehot, axis=-1))) * living)
    dlogits = (powers / totals[:, None] - onehot) * living[:, None] / count
    dnormed = lax.dot_general(dlogits, head_wide, (((1,), (1,)), ((), ())), precision=lax.Precision.HIGHEST, preferred_element_type=jnp.float32)
    dhidden = (inverse * (dnormed - normed * lax.optimization_barrier(jnp.mean(dnormed * normed, axis=-1, keepdims=True)))).astype(jnp.bfloat16)
    grad_up = contract_rows(active, dhidden)
    dactive = lax.dot_general(dhidden, up_low, (((1,), (1,)), ((), ())), preferred_element_type=jnp.float32)
    sigmoid = jax.nn.sigmoid(middle)
    dmiddle = (dactive * sigmoid * (1.0 + middle * (1.0 - sigmoid))).astype(jnp.bfloat16)
    grad_down = jnp.stack([contract_rows(window, dmiddle) for window in windows])
    grad_down = grad_down.reshape(3, 3, grids.shape[3], down_low.shape[3])
    return (loss_sum, grad_down, grad_up)

def step_scale(squares, entries):
    return 0.004 * lax.rsqrt(squares / entries + 1e-06)

def reference(feats, targets, task_of, counts, down_w, up_w, head):

    def one_task(inputs):
        group, down, upper, count = inputs
        order = jnp.argsort((task_of != group).astype(jnp.int32), stable=True)[:GROUP_MOST]
        chosen = task_of[order] == group
        grids = jnp.where(chosen[:, None, None, None], feats[order], jnp.zeros((), jnp.bfloat16))
        labels = jnp.where(chosen[:, None], targets[order], jnp.int32(-1)).astype(jnp.int32)
        scaled = count.astype(jnp.float32)
        collected = []
        for update_round in range(TRAIN_STEPS):
            loss_sum, grad_down, grad_up = train_pass(grids, labels, down.astype(jnp.bfloat16), upper.astype(jnp.bfloat16), head, scaled)
            scale = step_scale(jnp.sum(grad_down * grad_down) + jnp.sum(grad_up * grad_up), 10.0 * CHANNELS * INNER)
            down = down - scale * grad_down
            upper = upper - scale * grad_up
            collected.append(loss_sum / (scaled * GRID_CELLS))
        return (down, upper, jnp.stack(collected))
    down_new, up_new, losses = lax.map(one_task, (jnp.arange(ALL_TASKS, dtype=jnp.int32), down_w, up_w, counts))
    return (down_new, up_new, losses)
```

```python
import jax
import jax.numpy as jnp
from jax import lax
from jax.sharding import PartitionSpec as P

CHANNELS = 512
INNER = 256
TRAIN_STEPS = 2


def shifted_windows(grids):
    count_rows = grids.shape[0]
    side = grids.shape[1]
    padded = jnp.pad(grids, ((0, 0), (1, 1), (1, 1), (0, 0)))
    windows = []
    for offset_index in range(9):
        row_shift = offset_index // 3
        col_shift = offset_index % 3
        window = padded[:, row_shift : row_shift + side, col_shift : col_shift + side, :]
        windows.append(window.reshape(count_rows * side * side, grids.shape[3]))
    return windows


def contract_rows(left, right):
    return lax.dot_general(
        left, right, (((0,), (0,)), ((), ())), preferred_element_type=jnp.float32
    )


def train_pass(grids, labels, down_low, up_low, head, count):
    windows = shifted_windows(grids)
    flat_rows = windows[0].shape[0]
    middle = jnp.zeros((flat_rows, down_low.shape[3]), jnp.float32)
    for offset_index in range(9):
        middle = middle + jnp.dot(
            windows[offset_index],
            down_low[offset_index // 3, offset_index % 3],
            preferred_element_type=jnp.float32,
        )
    active = jax.nn.silu(middle).astype(jnp.bfloat16)
    hidden = grids.reshape(flat_rows, grids.shape[3]).astype(jnp.float32) + jnp.dot(
        active, up_low, preferred_element_type=jnp.float32
    )
    inverse = lax.rsqrt(jnp.mean(hidden * hidden, axis=-1, keepdims=True) + 1e-06)
    normed = hidden * inverse
    head_wide = head.astype(jnp.float32)
    logits = jnp.dot(
        normed, head_wide, precision=lax.Precision.HIGHEST, preferred_element_type=jnp.float32
    )
    flat_labels = labels.reshape(flat_rows)
    living = (flat_labels >= 0).astype(jnp.float32)
    onehot = (flat_labels[:, None] == jnp.arange(head.shape[1], dtype=jnp.int32)[None, :]).astype(
        jnp.float32
    )
    powers = jnp.exp(logits)
    totals = jnp.sum(powers, axis=-1)
    loss_sum = jnp.sum((jnp.log(totals) - jnp.sum(logits * onehot, axis=-1)) * living)
    dlogits = (powers / totals[:, None] - onehot) * living[:, None] / count
    dnormed = lax.dot_general(
        dlogits,
        head_wide,
        (((1,), (1,)), ((), ())),
        precision=lax.Precision.HIGHEST,
        preferred_element_type=jnp.float32,
    )
    dhidden = (
        inverse * (dnormed - normed * jnp.mean(dnormed * normed, axis=-1, keepdims=True))
    ).astype(jnp.bfloat16)
    grad_up = contract_rows(active, dhidden)
    dactive = lax.dot_general(
        dhidden, up_low, (((1,), (1,)), ((), ())), preferred_element_type=jnp.float32
    )
    sigmoid = jax.nn.sigmoid(middle)
    dmiddle = (dactive * sigmoid * (1.0 + middle * (1.0 - sigmoid))).astype(jnp.bfloat16)
    grad_down = jnp.stack([contract_rows(window, dmiddle) for window in windows])
    grad_down = grad_down.reshape(3, 3, grids.shape[3], down_low.shape[3])
    return (loss_sum, grad_down, grad_up)


def step_scale(squares, entries):
    return 0.004 * lax.rsqrt(squares / entries + 1e-06)


def shards(feats, targets, task_of, counts, down_w, up_w, head):
    groups = lax.axis_size("task")
    peers = lax.axis_size("ex")
    sources = feats.shape[0]
    side = feats.shape[1]
    chans = feats.shape[3]
    cells = side * side
    bucket = (2 * sources + groups - 1) // groups
    holding = 2 * sources
    order = jnp.arange(sources, dtype=jnp.int32)
    earlier = (task_of[:, None] == task_of[None, :]) & (order[None, :] < order[:, None])
    position = jnp.sum(earlier.astype(jnp.int32), axis=1)
    send_feats = (
        jnp.zeros((groups, bucket, side, side, chans), jnp.bfloat16)
        .at[task_of, position]
        .set(feats)
    )
    send_labels = (
        jnp.full((groups, bucket, cells), -1.0, jnp.bfloat16)
        .at[task_of, position]
        .set(targets.astype(jnp.bfloat16))
    )
    come_feats, come_labels = (
        lax.all_to_all(send_feats, "task", split_axis=0, concat_axis=0, tiled=True),
        lax.all_to_all(send_labels, "task", split_axis=0, concat_axis=0, tiled=True),
    )
    held_feats = come_feats.reshape(groups * bucket, side, side, chans)
    held_labels = come_labels.reshape(groups * bucket, cells).astype(jnp.int32)
    count = counts[0].astype(jnp.float32)
    entries = 10.0 * CHANNELS * INNER
    ex_place = lax.axis_index("ex")
    part_chans = down_w.shape[3] // peers
    part_inner = up_w.shape[1] // peers
    collected = []
    down_low = down_w[0].astype(jnp.bfloat16)
    upper_low = up_w[0].astype(jnp.bfloat16)
    down_own = lax.dynamic_slice_in_dim(down_w[0], ex_place * part_chans, part_chans, 2)
    up_own = lax.dynamic_slice_in_dim(up_w[0], ex_place * part_inner, part_inner, 0)
    for update_round in range(TRAIN_STEPS):
        loss_sum, grad_down, grad_up = train_pass(
            held_feats, held_labels, down_low, upper_low, head, count
        )
        grad_down = lax.psum_scatter(grad_down, "ex", scatter_dimension=2, tiled=True)
        grad_up = lax.psum_scatter(grad_up, "ex", scatter_dimension=0, tiled=True)
        squares = jnp.sum(grad_down * grad_down) + jnp.sum(grad_up * grad_up)
        totals = lax.psum(jnp.stack([squares, loss_sum]), "ex")
        scale = step_scale(totals[0], entries)
        down_own = down_own - scale * grad_down
        up_own = up_own - scale * grad_up
        collected.append(totals[1] / (count * cells))
        if update_round + 1 < TRAIN_STEPS:
            down_low = lax.all_gather(down_own.astype(jnp.bfloat16), "ex", axis=2, tiled=True)
            upper_low = lax.all_gather(up_own.astype(jnp.bfloat16), "ex", axis=0, tiled=True)
    return (down_own[None], up_own[None], jnp.stack(collected)[None])


def solution(mesh):
    placed = (
        P(("task", "ex"), None, None, None),
        P(("task", "ex"), None),
        P(("task", "ex")),
        P("task"),
        P("task", None, None, None, None),
        P("task", None, None),
        P(),
    )
    return jax.shard_map(
        shards,
        mesh=mesh,
        in_specs=placed,
        out_specs=(P("task", None, None, "ex", None), P("task", "ex", None), P("task", None)),
        check_vma=False,
    )
```

```python
import jax
import jax.numpy as jnp
from jax import lax
from jax.sharding import PartitionSpec as P

CHANNELS = 512
INNER = 256
TRAIN_STEPS = 2


def shifted_windows(grids):
    count_rows = grids.shape[0]
    side = grids.shape[1]
    padded = jnp.pad(grids, ((0, 0), (1, 1), (1, 1), (0, 0)))
    windows = []
    for offset_index in range(9):
        row_shift = offset_index // 3
        col_shift = offset_index % 3
        window = padded[:, row_shift : row_shift + side, col_shift : col_shift + side, :]
        windows.append(window.reshape(count_rows * side * side, grids.shape[3]))
    return windows


def contract_rows(left, right):
    return lax.dot_general(
        left, right, (((0,), (0,)), ((), ())), preferred_element_type=jnp.float32
    )


def train_pass(grids, labels, down_low, up_low, head, count):
    windows = shifted_windows(grids)
    flat_rows = windows[0].shape[0]
    middle = jnp.zeros((flat_rows, down_low.shape[3]), jnp.float32)
    for offset_index in range(9):
        middle = middle + jnp.dot(
            windows[offset_index],
            down_low[offset_index // 3, offset_index % 3],
            preferred_element_type=jnp.float32,
        )
    active = jax.nn.silu(middle).astype(jnp.bfloat16)
    hidden = grids.reshape(flat_rows, grids.shape[3]).astype(jnp.float32) + jnp.dot(
        active, up_low, preferred_element_type=jnp.float32
    )
    inverse = lax.rsqrt(jnp.mean(hidden * hidden, axis=-1, keepdims=True) + 1e-06)
    normed = hidden * inverse
    head_wide = head.astype(jnp.float32)
    logits = jnp.dot(
        normed, head_wide, precision=lax.Precision.HIGHEST, preferred_element_type=jnp.float32
    )
    flat_labels = labels.reshape(flat_rows)
    living = (flat_labels >= 0).astype(jnp.float32)
    onehot = (flat_labels[:, None] == jnp.arange(head.shape[1], dtype=jnp.int32)[None, :]).astype(
        jnp.float32
    )
    powers = jnp.exp(logits)
    totals = jnp.sum(powers, axis=-1)
    loss_sum = jnp.sum((jnp.log(totals) - jnp.sum(logits * onehot, axis=-1)) * living)
    dlogits = (powers / totals[:, None] - onehot) * living[:, None] / count
    dnormed = lax.dot_general(
        dlogits,
        head_wide,
        (((1,), (1,)), ((), ())),
        precision=lax.Precision.HIGHEST,
        preferred_element_type=jnp.float32,
    )
    dhidden = (
        inverse * (dnormed - normed * jnp.mean(dnormed * normed, axis=-1, keepdims=True))
    ).astype(jnp.bfloat16)
    grad_up = contract_rows(active, dhidden)
    dactive = lax.dot_general(
        dhidden, up_low, (((1,), (1,)), ((), ())), preferred_element_type=jnp.float32
    )
    sigmoid = jax.nn.sigmoid(middle)
    dmiddle = (dactive * sigmoid * (1.0 + middle * (1.0 - sigmoid))).astype(jnp.bfloat16)
    grad_down = jnp.stack([contract_rows(window, dmiddle) for window in windows])
    grad_down = grad_down.reshape(3, 3, grids.shape[3], down_low.shape[3])
    return (loss_sum, grad_down, grad_up)


def step_scale(squares, entries):
    return 0.004 * lax.rsqrt(squares / entries + 1e-06)


def partner_swap(value, bit, peers):
    return lax.ppermute(value, "ex", perm=[(i, i ^ (1 << bit)) for i in range(peers)])


def halve_sum(value, axis, bit, place, peers):
    mine = (place >> bit) & 1
    keep = lax.dynamic_index_in_dim(value, mine, axis, keepdims=False)
    give = lax.dynamic_index_in_dim(value, 1 - mine, axis, keepdims=False)
    return keep + partner_swap(give, bit, peers)


def double_join(value, axis, bit, place, peers):
    mine = (place >> bit) & 1
    other = partner_swap(value, bit, peers)
    first = jnp.where(mine == 0, value, other)
    second = jnp.where(mine == 0, other, value)
    return jnp.stack([first, second], axis=axis)


def shards(feats, targets, task_of, counts, down_w, up_w, head):
    groups = lax.axis_size("task")
    peers = lax.axis_size("ex")
    levels = peers.bit_length() - 1
    sources = feats.shape[0]
    side = feats.shape[1]
    chans = feats.shape[3]
    cells = side * side
    bucket = (2 * sources + groups - 1) // groups
    order = jnp.arange(sources, dtype=jnp.int32)
    earlier = (task_of[:, None] == task_of[None, :]) & (order[None, :] < order[:, None])
    position = jnp.sum(earlier.astype(jnp.int32), axis=1)
    send_feats = (
        jnp.zeros((groups, bucket, side, side, chans), jnp.bfloat16)
        .at[task_of, position]
        .set(feats)
    )
    send_labels = (
        jnp.full((groups, bucket, cells), -1.0, jnp.bfloat16)
        .at[task_of, position]
        .set(targets.astype(jnp.bfloat16))
    )
    come_feats, come_labels = (
        lax.all_to_all(send_feats, "task", split_axis=0, concat_axis=0, tiled=True),
        lax.all_to_all(send_labels, "task", split_axis=0, concat_axis=0, tiled=True),
    )
    held_feats = come_feats.reshape(groups * bucket, side, side, chans)
    held_labels = come_labels.reshape(groups * bucket, cells).astype(jnp.int32)
    count = counts[0].astype(jnp.float32)
    entries = 10.0 * CHANNELS * INNER
    place = lax.axis_index("ex")
    part_chans = down_w.shape[3] // peers
    part_inner = up_w.shape[1] // peers
    inner = down_w.shape[4]
    collected = []
    down_low = down_w[0].astype(jnp.bfloat16)
    upper_low = up_w[0].astype(jnp.bfloat16)
    down_own = lax.dynamic_slice_in_dim(down_w[0], place * part_chans, part_chans, 2)
    up_own = lax.dynamic_slice_in_dim(up_w[0], place * part_inner, part_inner, 0)
    bits_shape = (2,) * levels
    for update_round in range(TRAIN_STEPS):
        loss_sum, grad_down, grad_up = train_pass(
            held_feats, held_labels, down_low, upper_low, head, count
        )
        grad_down = grad_down.reshape((3, 3) + bits_shape + (part_chans, inner))
        grad_up = grad_up.reshape(bits_shape + (part_inner, up_w.shape[2]))
        for bit in range(levels):
            grad_down = halve_sum(grad_down, 2 + levels - 1 - bit, bit, place, peers)
            grad_up = halve_sum(grad_up, levels - 1 - bit, bit, place, peers)
        squares = jnp.sum(grad_down * grad_down) + jnp.sum(grad_up * grad_up)
        totals = jnp.stack([squares, loss_sum])
        for bit in range(levels):
            totals = totals + partner_swap(totals, bit, peers)
        scale = step_scale(totals[0], entries)
        down_own = down_own - scale * grad_down
        up_own = up_own - scale * grad_up
        collected.append(totals[1] / (count * cells))
        if update_round + 1 < TRAIN_STEPS:
            down_low = down_own.astype(jnp.bfloat16)
            upper_low = up_own.astype(jnp.bfloat16)
            for step_index, bit in enumerate(reversed(range(levels))):
                down_low = double_join(down_low, 2 + step_index, bit, place, peers)
                upper_low = double_join(upper_low, step_index, bit, place, peers)
            down_low = down_low.reshape(down_w.shape[1:])
            upper_low = upper_low.reshape(up_w.shape[1:])
    return (down_own[None], up_own[None], jnp.stack(collected)[None])


def solution(mesh):
    placed = (
        P(("task", "ex"), None, None, None),
        P(("task", "ex"), None),
        P(("task", "ex")),
        P("task"),
        P("task", None, None, None, None),
        P("task", None, None),
        P(),
    )
    return jax.shard_map(
        shards,
        mesh=mesh,
        in_specs=placed,
        out_specs=(P("task", None, None, "ex", None), P("task", "ex", None), P("task", None)),
        check_vma=False,
    )
```

```python
import jax
import jax.numpy as jnp
from jax import lax
from jax.sharding import PartitionSpec as P

CHANNELS = 512
INNER = 256
TRAIN_STEPS = 2


def shifted_windows(grids):
    count_rows = grids.shape[0]
    side = grids.shape[1]
    padded = jnp.pad(grids, ((0, 0), (1, 1), (1, 1), (0, 0)))
    windows = []
    for offset_index in range(9):
        row_shift = offset_index // 3
        col_shift = offset_index % 3
        window = padded[:, row_shift : row_shift + side, col_shift : col_shift + side, :]
        windows.append(window.reshape(count_rows * side * side, grids.shape[3]))
    return windows


def contract_rows(left, right):
    return lax.dot_general(
        left, right, (((0,), (0,)), ((), ())), preferred_element_type=jnp.float32
    )


def train_pass(grids, labels, down_low, up_low, head, count):
    windows = shifted_windows(grids)
    flat_rows = windows[0].shape[0]
    middle = jnp.zeros((flat_rows, down_low.shape[3]), jnp.float32)
    for offset_index in range(9):
        middle = middle + jnp.dot(
            windows[offset_index],
            down_low[offset_index // 3, offset_index % 3],
            preferred_element_type=jnp.float32,
        )
    active = jax.nn.silu(middle).astype(jnp.bfloat16)
    hidden = grids.reshape(flat_rows, grids.shape[3]).astype(jnp.float32) + jnp.dot(
        active, up_low, preferred_element_type=jnp.float32
    )
    inverse = lax.rsqrt(jnp.mean(hidden * hidden, axis=-1, keepdims=True) + 1e-06)
    normed = hidden * inverse
    head_wide = head.astype(jnp.float32)
    logits = jnp.dot(
        normed, head_wide, precision=lax.Precision.HIGHEST, preferred_element_type=jnp.float32
    )
    flat_labels = labels.reshape(flat_rows)
    living = (flat_labels >= 0).astype(jnp.float32)
    onehot = (flat_labels[:, None] == jnp.arange(head.shape[1], dtype=jnp.int32)[None, :]).astype(
        jnp.float32
    )
    powers = jnp.exp(logits)
    totals = jnp.sum(powers, axis=-1)
    loss_sum = jnp.sum((jnp.log(totals) - jnp.sum(logits * onehot, axis=-1)) * living)
    dlogits = (powers / totals[:, None] - onehot) * living[:, None] / count
    dnormed = lax.dot_general(
        dlogits,
        head_wide,
        (((1,), (1,)), ((), ())),
        precision=lax.Precision.HIGHEST,
        preferred_element_type=jnp.float32,
    )
    dhidden = (
        inverse * (dnormed - normed * jnp.mean(dnormed * normed, axis=-1, keepdims=True))
    ).astype(jnp.bfloat16)
    grad_up = contract_rows(active, dhidden)
    dactive = lax.dot_general(
        dhidden, up_low, (((1,), (1,)), ((), ())), preferred_element_type=jnp.float32
    )
    sigmoid = jax.nn.sigmoid(middle)
    dmiddle = (dactive * sigmoid * (1.0 + middle * (1.0 - sigmoid))).astype(jnp.bfloat16)
    grad_down = jnp.stack([contract_rows(window, dmiddle) for window in windows])
    grad_down = grad_down.reshape(3, 3, grids.shape[3], down_low.shape[3])
    return (loss_sum, grad_down, grad_up)


def step_scale(squares, entries):
    return 0.004 * lax.rsqrt(squares / entries + 1e-06)


def partner_swap(value, pairs):
    return lax.ppermute(value, "ex", perm=pairs)


def stage_pairs(bits_of, peers):
    return [(i, i ^ (1 << bits_of[i % 2])) for i in range(peers)]


def halve_sum(value, axis, bit, pairs, place):
    mine = (place >> bit) & 1
    keep = lax.dynamic_index_in_dim(value, mine, axis, keepdims=False)
    give = lax.dynamic_index_in_dim(value, 1 - mine, axis, keepdims=False)
    return keep + partner_swap(give, pairs)


def double_join(value, axis, bit, pairs, place):
    mine = (place >> bit) & 1
    other = partner_swap(value, pairs)
    first = jnp.where(mine == 0, value, other)
    second = jnp.where(mine == 0, other, value)
    return jnp.stack([first, second], axis=axis)


def swap_bit_axes(value, lead, levels):
    order = list(range(value.ndim))
    order[lead : lead + 4] = [lead + 2, lead + 3, lead, lead + 1]
    return jnp.transpose(value, order)


def shards(feats, targets, task_of, counts, down_w, up_w, head):
    groups = lax.axis_size("task")
    peers = lax.axis_size("ex")
    levels = peers.bit_length() - 1
    sources = feats.shape[0]
    side = feats.shape[1]
    chans = feats.shape[3]
    cells = side * side
    bucket = (2 * sources + groups - 1) // groups
    order = jnp.arange(sources, dtype=jnp.int32)
    earlier = (task_of[:, None] == task_of[None, :]) & (order[None, :] < order[:, None])
    position = jnp.sum(earlier.astype(jnp.int32), axis=1)
    send_feats = (
        jnp.zeros((groups, bucket, side, side, chans), jnp.bfloat16)
        .at[task_of, position]
        .set(feats)
    )
    send_labels = (
        jnp.full((groups, bucket, cells), -1.0, jnp.bfloat16)
        .at[task_of, position]
        .set(targets.astype(jnp.bfloat16))
    )
    come_feats, come_labels = (
        lax.all_to_all(send_feats, "task", split_axis=0, concat_axis=0, tiled=True),
        lax.all_to_all(send_labels, "task", split_axis=0, concat_axis=0, tiled=True),
    )
    held_feats = come_feats.reshape(groups * bucket, side, side, chans)
    held_labels = come_labels.reshape(groups * bucket, cells).astype(jnp.int32)
    count = counts[0].astype(jnp.float32)
    entries = 10.0 * CHANNELS * INNER
    place = lax.axis_index("ex")
    part_chans = down_w.shape[3] // peers
    part_inner = up_w.shape[1] // peers
    inner = down_w.shape[4]
    collected = []
    down_low = down_w[0].astype(jnp.bfloat16)
    upper_low = up_w[0].astype(jnp.bfloat16)
    down_own = lax.dynamic_slice_in_dim(down_w[0], place * part_chans, part_chans, 2)
    up_own = lax.dynamic_slice_in_dim(up_w[0], place * part_inner, part_inner, 0)
    bits_shape = (2,) * levels
    core = place % 2
    second_core = core == 1
    orders = ([0, 1, 2, 3, 4], [0, 3, 4, 1, 2])
    for update_round in range(TRAIN_STEPS):
        loss_sum, grad_down, grad_up = train_pass(
            held_feats, held_labels, down_low, upper_low, head, count
        )
        grad_down = grad_down.reshape((3, 3) + bits_shape + (part_chans, inner))
        grad_up = grad_up.reshape(bits_shape + (part_inner, up_w.shape[2]))
        for stage in range(levels):
            if stage == 1:
                grad_down = jnp.where(second_core, swap_bit_axes(grad_down, 2, levels), grad_down)
                grad_up = jnp.where(second_core, swap_bit_axes(grad_up, 0, levels), grad_up)
            bits_of = (orders[0][stage], orders[1][stage])
            pairs = stage_pairs(bits_of, peers)
            bit = jnp.where(second_core, bits_of[1], bits_of[0])
            grad_down = halve_sum(grad_down, 2 + levels - 1 - stage, bit, pairs, place)
            grad_up = halve_sum(grad_up, levels - 1 - stage, bit, pairs, place)
        squares = jnp.sum(grad_down * grad_down) + jnp.sum(grad_up * grad_up)
        totals = jnp.stack([squares, loss_sum])
        for bit in range(levels):
            totals = totals + partner_swap(totals, stage_pairs((bit, bit), peers))
        scale = step_scale(totals[0], entries)
        down_own = down_own - scale * grad_down
        up_own = up_own - scale * grad_up
        collected.append(totals[1] / (count * cells))
        if update_round + 1 < TRAIN_STEPS:
            down_low = down_own.astype(jnp.bfloat16)
            upper_low = up_own.astype(jnp.bfloat16)
            for step_index in range(levels):
                stage = levels - 1 - step_index
                if stage == 0:
                    down_low = jnp.where(second_core, swap_bit_axes(down_low, 2, levels), down_low)
                    upper_low = jnp.where(second_core, swap_bit_axes(upper_low, 0, levels), upper_low)
                bits_of = (orders[0][stage], orders[1][stage])
                pairs = stage_pairs(bits_of, peers)
                bit = jnp.where(second_core, bits_of[1], bits_of[0])
                down_low = double_join(down_low, 2 + step_index, bit, pairs, place)
                upper_low = double_join(upper_low, step_index, bit, pairs, place)
            down_low = down_low.reshape(down_w.shape[1:])
            upper_low = upper_low.reshape(up_w.shape[1:])
    return (down_own[None], up_own[None], jnp.stack(collected)[None])


def solution(mesh):
    placed = (
        P(("task", "ex"), None, None, None),
        P(("task", "ex"), None),
        P(("task", "ex")),
        P("task"),
        P("task", None, None, None, None),
        P("task", None, None),
        P(),
    )
    return jax.shard_map(
        shards,
        mesh=mesh,
        in_specs=placed,
        out_specs=(P("task", None, None, "ex", None), P("task", "ex", None), P("task", None)),
        check_vma=False,
    )
```

```python
import jax
import jax.numpy as jnp
from jax import lax
from jax.sharding import PartitionSpec as P

CHANNELS = 512
INNER = 256
TRAIN_STEPS = 2


def shifted_windows(grids):
    count_rows = grids.shape[0]
    side = grids.shape[1]
    padded = jnp.pad(grids, ((0, 0), (1, 1), (1, 1), (0, 0)))
    windows = []
    for offset_index in range(9):
        row_shift = offset_index // 3
        col_shift = offset_index % 3
        window = padded[:, row_shift : row_shift + side, col_shift : col_shift + side, :]
        windows.append(window.reshape(count_rows * side * side, grids.shape[3]))
    return windows


def contract_rows(left, right):
    return lax.dot_general(
        left, right, (((0,), (0,)), ((), ())), preferred_element_type=jnp.float32
    )


def train_pass(grids, labels, down_low, up_low, head, count):
    windows = shifted_windows(grids)
    flat_rows = windows[0].shape[0]
    middle = jnp.zeros((flat_rows, down_low.shape[3]), jnp.float32)
    for offset_index in range(9):
        middle = middle + jnp.dot(
            windows[offset_index],
            down_low[offset_index // 3, offset_index % 3],
            preferred_element_type=jnp.float32,
        )
    active = jax.nn.silu(middle).astype(jnp.bfloat16)
    hidden = grids.reshape(flat_rows, grids.shape[3]).astype(jnp.float32) + jnp.dot(
        active, up_low, preferred_element_type=jnp.float32
    )
    inverse = lax.rsqrt(jnp.mean(hidden * hidden, axis=-1, keepdims=True) + 1e-06)
    normed = hidden * inverse
    head_wide = head.astype(jnp.float32)
    logits = jnp.dot(
        normed, head_wide, precision=lax.Precision.HIGHEST, preferred_element_type=jnp.float32
    )
    flat_labels = labels.reshape(flat_rows)
    living = (flat_labels >= 0).astype(jnp.float32)
    onehot = (flat_labels[:, None] == jnp.arange(head.shape[1], dtype=jnp.int32)[None, :]).astype(
        jnp.float32
    )
    powers = jnp.exp(logits)
    totals = jnp.sum(powers, axis=-1)
    loss_sum = jnp.sum((jnp.log(totals) - jnp.sum(logits * onehot, axis=-1)) * living)
    dlogits = (powers / totals[:, None] - onehot) * living[:, None] / count
    dnormed = lax.dot_general(
        dlogits,
        head_wide,
        (((1,), (1,)), ((), ())),
        precision=lax.Precision.HIGHEST,
        preferred_element_type=jnp.float32,
    )
    dhidden = (
        inverse * (dnormed - normed * jnp.mean(dnormed * normed, axis=-1, keepdims=True))
    ).astype(jnp.bfloat16)
    grad_up = contract_rows(active, dhidden)
    dactive = lax.dot_general(
        dhidden, up_low, (((1,), (1,)), ((), ())), preferred_element_type=jnp.float32
    )
    sigmoid = jax.nn.sigmoid(middle)
    dmiddle = (dactive * sigmoid * (1.0 + middle * (1.0 - sigmoid))).astype(jnp.bfloat16)
    grad_down = jnp.stack([contract_rows(window, dmiddle) for window in windows])
    grad_down = grad_down.reshape(3, 3, grids.shape[3], down_low.shape[3])
    return (loss_sum, grad_down, grad_up)


def step_scale(squares, entries):
    return 0.004 * lax.rsqrt(squares / entries + 1e-06)


def partner_swap(value, pairs):
    return lax.ppermute(value, "ex", perm=pairs)


def stage_pairs(bits_of, peers):
    return [(i, i ^ (1 << bits_of[i % 2])) for i in range(peers)]


def swap_bit_axes(value):
    order = list(range(value.ndim))
    order[:4] = [2, 3, 0, 1]
    return jnp.transpose(value, order)


STAGE_BITS = ((0, 1, 2, 3, 4), (0, 3, 4, 1, 2))


def scatter_sum(packed, place, second_core, levels, peers):
    for stage in range(levels):
        if stage == 1:
            packed = jnp.where(second_core, swap_bit_axes(packed), packed)
        bits_of = (STAGE_BITS[0][stage], STAGE_BITS[1][stage])
        bit = jnp.where(second_core, bits_of[1], bits_of[0])
        mine = (place >> bit) & 1
        axis = levels - 1 - stage
        keep = lax.dynamic_index_in_dim(packed, mine, axis, keepdims=False)
        give = lax.dynamic_index_in_dim(packed, 1 - mine, axis, keepdims=False)
        packed = keep + partner_swap(give, stage_pairs(bits_of, peers))
    return packed


def gather_all(block, place, second_core, levels, peers):
    for step_index in range(levels):
        stage = levels - 1 - step_index
        if stage == 0:
            block = jnp.where(second_core, swap_bit_axes(block), block)
        bits_of = (STAGE_BITS[0][stage], STAGE_BITS[1][stage])
        bit = jnp.where(second_core, bits_of[1], bits_of[0])
        mine = (place >> bit) & 1
        other = partner_swap(block, stage_pairs(bits_of, peers))
        first = jnp.where(mine == 0, block, other)
        second = jnp.where(mine == 0, other, block)
        block = jnp.stack([first, second], axis=step_index)
    return block


def pack_grads(grad_down, grad_up, peers, spare):
    lanes = 128
    down_rows = grad_down.reshape(3, 3, peers, -1, grad_down.shape[3])
    down_rows = jnp.transpose(down_rows, (2, 0, 1, 3, 4)).reshape(peers, -1, lanes)
    up_rows = grad_up.reshape(peers, -1, lanes)
    parts = [down_rows, up_rows]
    if spare is not None:
        parts.append(spare)
    return jnp.concatenate(parts, axis=1)


def shards(feats, targets, task_of, counts, down_w, up_w, head):
    groups = lax.axis_size("task")
    peers = lax.axis_size("ex")
    levels = peers.bit_length() - 1
    sources = feats.shape[0]
    side = feats.shape[1]
    chans = feats.shape[3]
    cells = side * side
    bucket = (2 * sources + groups - 1) // groups
    order = jnp.arange(sources, dtype=jnp.int32)
    earlier = (task_of[:, None] == task_of[None, :]) & (order[None, :] < order[:, None])
    position = jnp.sum(earlier.astype(jnp.int32), axis=1)
    send_feats = (
        jnp.zeros((groups, bucket, side, side, chans), jnp.bfloat16)
        .at[task_of, position]
        .set(feats)
    )
    send_labels = (
        jnp.full((groups, bucket, cells), -1.0, jnp.bfloat16)
        .at[task_of, position]
        .set(targets.astype(jnp.bfloat16))
    )
    come_feats, come_labels = (
        lax.all_to_all(send_feats, "task", split_axis=0, concat_axis=0, tiled=True),
        lax.all_to_all(send_labels, "task", split_axis=0, concat_axis=0, tiled=True),
    )
    held_feats = come_feats.reshape(groups * bucket, side, side, chans)
    held_labels = come_labels.reshape(groups * bucket, cells).astype(jnp.int32)
    count = counts[0].astype(jnp.float32)
    entries = 10.0 * CHANNELS * INNER
    place = lax.axis_index("ex")
    part_chans = down_w.shape[3] // peers
    part_inner = up_w.shape[1] // peers
    inner = down_w.shape[4]
    outer = up_w.shape[2]
    lanes = 128
    down_span = 9 * part_chans * inner // lanes
    up_span = part_inner * outer // lanes
    second_core = (place % 2) == 1
    bits_shape = (2,) * levels
    spare_rows = 8

    loss_sum, grad_down, grad_up = train_pass(
        held_feats, held_labels, down_w[0].astype(jnp.bfloat16), up_w[0].astype(jnp.bfloat16), head, count
    )
    row_ids = lax.broadcasted_iota(jnp.int32, (peers, spare_rows, lanes), 0)
    col_ids = lax.broadcasted_iota(jnp.int32, (peers, spare_rows, lanes), 2)
    first_cell = (row_ids == 0) & (col_ids == 0)
    spare = jnp.where(first_cell & (lax.broadcasted_iota(jnp.int32, (peers, spare_rows, lanes), 1) == 0), loss_sum, 0.0)
    packed = pack_grads(grad_down, grad_up, peers, spare)
    packed = packed.reshape(bits_shape + packed.shape[1:])
    block = scatter_sum(packed, place, second_core, levels, peers)
    full = gather_all(block, place, second_core, levels, peers).reshape((peers,) + block.shape)
    full_down = full[:, :down_span].reshape(peers, 3, 3, part_chans, inner)
    full_down = jnp.transpose(full_down, (1, 2, 0, 3, 4)).reshape(down_w.shape[1:])
    full_up = full[:, down_span : down_span + up_span].reshape(up_w.shape[1:])
    loss_first = full[0, down_span + up_span, 0]
    squares = jnp.sum(full_down * full_down) + jnp.sum(full_up * full_up)
    scale = step_scale(squares, entries)
    down_next = down_w[0] - scale * full_down
    up_next = up_w[0] - scale * full_up
    down_own = lax.dynamic_slice_in_dim(down_next, place * part_chans, part_chans, 2)
    up_own = lax.dynamic_slice_in_dim(up_next, place * part_inner, part_inner, 0)

    loss_sum, grad_down, grad_up = train_pass(
        held_feats, held_labels, down_next.astype(jnp.bfloat16), up_next.astype(jnp.bfloat16), head, count
    )
    packed = pack_grads(grad_down, grad_up, peers, None)
    packed = packed.reshape(bits_shape + packed.shape[1:])
    block = scatter_sum(packed, place, second_core, levels, peers)
    shard_down = block[:down_span].reshape(down_own.shape)
    shard_up = block[down_span:].reshape(up_own.shape)
    totals = jnp.stack([jnp.sum(shard_down * shard_down) + jnp.sum(shard_up * shard_up), loss_sum])
    for bit in range(levels):
        totals = totals + partner_swap(totals, stage_pairs((bit, bit), peers))
    scale = step_scale(totals[0], entries)
    down_own = down_own - scale * shard_down
    up_own = up_own - scale * shard_up
    losses = jnp.stack([loss_first, totals[1]]) / (count * cells)
    return (down_own[None], up_own[None], losses[None])


def solution(mesh):
    placed = (
        P(("task", "ex"), None, None, None),
        P(("task", "ex"), None),
        P(("task", "ex")),
        P("task"),
        P("task", None, None, None, None),
        P("task", None, None),
        P(),
    )
    return jax.shard_map(
        shards,
        mesh=mesh,
        in_specs=placed,
        out_specs=(P("task", None, None, "ex", None), P("task", "ex", None), P("task", None)),
        check_vma=False,
    )
```

```python
import jax
import jax.numpy as jnp
from jax import lax
from jax.sharding import PartitionSpec as P

CHANNELS = 512
INNER = 256
TRAIN_STEPS = 2


def shifted_windows(grids):
    count_rows = grids.shape[0]
    side = grids.shape[1]
    padded = jnp.pad(grids, ((0, 0), (1, 1), (1, 1), (0, 0)))
    windows = []
    for offset_index in range(9):
        row_shift = offset_index // 3
        col_shift = offset_index % 3
        window = padded[:, row_shift : row_shift + side, col_shift : col_shift + side, :]
        windows.append(window.reshape(count_rows * side * side, grids.shape[3]))
    return windows


def contract_rows(left, right):
    return lax.dot_general(
        left, right, (((0,), (0,)), ((), ())), preferred_element_type=jnp.float32
    )


def train_pass(grids, labels, down_low, up_low, head, count):
    windows = shifted_windows(grids)
    flat_rows = windows[0].shape[0]
    middle = jnp.zeros((flat_rows, down_low.shape[3]), jnp.float32)
    for offset_index in range(9):
        middle = middle + jnp.dot(
            windows[offset_index],
            down_low[offset_index // 3, offset_index % 3],
            preferred_element_type=jnp.float32,
        )
    active = jax.nn.silu(middle).astype(jnp.bfloat16)
    hidden = grids.reshape(flat_rows, grids.shape[3]).astype(jnp.float32) + jnp.dot(
        active, up_low, preferred_element_type=jnp.float32
    )
    inverse = lax.rsqrt(jnp.mean(hidden * hidden, axis=-1, keepdims=True) + 1e-06)
    normed = hidden * inverse
    head_wide = head.astype(jnp.float32)
    logits = jnp.dot(
        normed, head_wide, precision=lax.Precision.HIGHEST, preferred_element_type=jnp.float32
    )
    flat_labels = labels.reshape(flat_rows)
    living = (flat_labels >= 0).astype(jnp.float32)
    onehot = (flat_labels[:, None] == jnp.arange(head.shape[1], dtype=jnp.int32)[None, :]).astype(
        jnp.float32
    )
    powers = jnp.exp(logits)
    totals = jnp.sum(powers, axis=-1)
    loss_sum = jnp.sum((jnp.log(totals) - jnp.sum(logits * onehot, axis=-1)) * living)
    dlogits = (powers / totals[:, None] - onehot) * living[:, None] / count
    dnormed = lax.dot_general(
        dlogits,
        head_wide,
        (((1,), (1,)), ((), ())),
        precision=lax.Precision.HIGHEST,
        preferred_element_type=jnp.float32,
    )
    dhidden = (
        inverse * (dnormed - normed * jnp.mean(dnormed * normed, axis=-1, keepdims=True))
    ).astype(jnp.bfloat16)
    grad_up = contract_rows(active, dhidden)
    dactive = lax.dot_general(
        dhidden, up_low, (((1,), (1,)), ((), ())), preferred_element_type=jnp.float32
    )
    sigmoid = jax.nn.sigmoid(middle)
    dmiddle = (dactive * sigmoid * (1.0 + middle * (1.0 - sigmoid))).astype(jnp.bfloat16)
    grad_down = jnp.stack([contract_rows(window, dmiddle) for window in windows])
    grad_down = grad_down.reshape(3, 3, grids.shape[3], down_low.shape[3])
    return (loss_sum, grad_down, grad_up)


def step_scale(squares, entries):
    return 0.004 * lax.rsqrt(squares / entries + 1e-06)


def partner_swap(value, pairs):
    return lax.ppermute(value, "ex", perm=pairs)


def stage_pairs(bits_of, peers):
    return [(i, i ^ (1 << bits_of[i % 2])) for i in range(peers)]


def halve_sum(value, axis, bit, pairs, place):
    mine = (place >> bit) & 1
    keep = lax.dynamic_index_in_dim(value, mine, axis, keepdims=False)
    give = lax.dynamic_index_in_dim(value, 1 - mine, axis, keepdims=False)
    return keep + partner_swap(give, pairs)


def double_join(value, axis, bit, pairs, place):
    mine = (place >> bit) & 1
    other = partner_swap(value, pairs)
    first = jnp.where(mine == 0, value, other)
    second = jnp.where(mine == 0, other, value)
    return jnp.stack([first, second], axis=axis)


def swap_bit_axes(value, lead, levels):
    order = list(range(value.ndim))
    order[lead : lead + 4] = [lead + 2, lead + 3, lead, lead + 1]
    return jnp.transpose(value, order)


def shards(feats, targets, task_of, counts, down_w, up_w, head):
    groups = lax.axis_size("task")
    peers = lax.axis_size("ex")
    levels = peers.bit_length() - 1
    sources = feats.shape[0]
    side = feats.shape[1]
    chans = feats.shape[3]
    cells = side * side
    bucket = (2 * sources + groups - 1) // groups
    order = jnp.arange(sources, dtype=jnp.int32)
    earlier = (task_of[:, None] == task_of[None, :]) & (order[None, :] < order[:, None])
    position = jnp.sum(earlier.astype(jnp.int32), axis=1)
    task_place = lax.axis_index("task")
    slot_ids = jnp.arange(bucket, dtype=jnp.int32)
    flat_feats = feats.reshape(sources, side * side * chans)
    bucket_feats = []
    bucket_labels = []
    for shift in range(groups):
        target_task = (task_place + shift) % groups
        picks = (task_of[None, :] == target_task) & (position[None, :] == slot_ids[:, None])
        chosen_feats = jnp.dot(
            picks.astype(jnp.bfloat16), flat_feats, preferred_element_type=jnp.float32
        ).astype(jnp.bfloat16)
        chosen_labels = jnp.sum(jnp.where(picks[:, :, None], targets[None, :, :], 0), axis=1)
        chosen_labels = jnp.where(jnp.any(picks, axis=1)[:, None], chosen_labels, -1)
        chosen_labels = chosen_labels.astype(jnp.bfloat16)
        if shift:
            pairs = [(t, (t + shift) % groups) for t in range(groups)]
            chosen_feats, chosen_labels = lax.ppermute(
                (chosen_feats, chosen_labels), "task", perm=pairs
            )
        bucket_feats.append(chosen_feats)
        bucket_labels.append(chosen_labels)
    held_feats = jnp.concatenate(bucket_feats, axis=0).reshape(groups * bucket, side, side, chans)
    held_labels = jnp.concatenate(bucket_labels, axis=0).astype(jnp.int32)
    count = counts[0].astype(jnp.float32)
    entries = 10.0 * CHANNELS * INNER
    place = lax.axis_index("ex")
    part_chans = down_w.shape[3] // peers
    part_inner = up_w.shape[1] // peers
    inner = down_w.shape[4]
    collected = []
    down_low = down_w[0].astype(jnp.bfloat16)
    upper_low = up_w[0].astype(jnp.bfloat16)
    down_own = lax.dynamic_slice_in_dim(down_w[0], place * part_chans, part_chans, 2)
    up_own = lax.dynamic_slice_in_dim(up_w[0], place * part_inner, part_inner, 0)
    bits_shape = (2,) * levels
    core = place % 2
    second_core = core == 1
    orders = ([0, 1, 2, 3, 4], [0, 3, 4, 1, 2])
    for update_round in range(TRAIN_STEPS):
        loss_sum, grad_down, grad_up = train_pass(
            held_feats, held_labels, down_low, upper_low, head, count
        )
        grad_down = grad_down.reshape((3, 3) + bits_shape + (part_chans, inner))
        grad_up = grad_up.reshape(bits_shape + (part_inner, up_w.shape[2]))
        for stage in range(levels):
            if stage == 1:
                grad_down = jnp.where(second_core, swap_bit_axes(grad_down, 2, levels), grad_down)
                grad_up = jnp.where(second_core, swap_bit_axes(grad_up, 0, levels), grad_up)
            bits_of = (orders[0][stage], orders[1][stage])
            pairs = stage_pairs(bits_of, peers)
            bit = jnp.where(second_core, bits_of[1], bits_of[0])
            grad_down = halve_sum(grad_down, 2 + levels - 1 - stage, bit, pairs, place)
            grad_up = halve_sum(grad_up, levels - 1 - stage, bit, pairs, place)
        squares = jnp.sum(grad_down * grad_down) + jnp.sum(grad_up * grad_up)
        totals = jnp.stack([squares, loss_sum])
        for bit in range(levels):
            totals = totals + partner_swap(totals, stage_pairs((bit, bit), peers))
        scale = step_scale(totals[0], entries)
        down_own = down_own - scale * grad_down
        up_own = up_own - scale * grad_up
        collected.append(totals[1] / (count * cells))
        if update_round + 1 < TRAIN_STEPS:
            down_low = down_own.astype(jnp.bfloat16)
            upper_low = up_own.astype(jnp.bfloat16)
            for step_index in range(levels):
                stage = levels - 1 - step_index
                if stage == 0:
                    down_low = jnp.where(second_core, swap_bit_axes(down_low, 2, levels), down_low)
                    upper_low = jnp.where(second_core, swap_bit_axes(upper_low, 0, levels), upper_low)
                bits_of = (orders[0][stage], orders[1][stage])
                pairs = stage_pairs(bits_of, peers)
                bit = jnp.where(second_core, bits_of[1], bits_of[0])
                down_low = double_join(down_low, 2 + step_index, bit, pairs, place)
                upper_low = double_join(upper_low, step_index, bit, pairs, place)
            down_low = down_low.reshape(down_w.shape[1:])
            upper_low = upper_low.reshape(up_w.shape[1:])
    return (down_own[None], up_own[None], jnp.stack(collected)[None])


def solution(mesh):
    placed = (
        P(("task", "ex"), None, None, None),
        P(("task", "ex"), None),
        P(("task", "ex")),
        P("task"),
        P("task", None, None, None, None),
        P("task", None, None),
        P(),
    )
    return jax.shard_map(
        shards,
        mesh=mesh,
        in_specs=placed,
        out_specs=(P("task", None, None, "ex", None), P("task", "ex", None), P("task", None)),
        check_vma=False,
    )
```

```python
import jax
import jax.numpy as jnp
from jax import lax
from jax.sharding import PartitionSpec as P

CHANNELS = 512
INNER = 256
TRAIN_STEPS = 2


def shifted_windows(grids):
    count_rows = grids.shape[0]
    side = grids.shape[1]
    padded = jnp.pad(grids, ((0, 0), (1, 1), (1, 1), (0, 0)))
    windows = []
    for offset_index in range(9):
        row_shift = offset_index // 3
        col_shift = offset_index % 3
        window = padded[:, row_shift : row_shift + side, col_shift : col_shift + side, :]
        windows.append(window.reshape(count_rows * side * side, grids.shape[3]))
    return windows


def contract_rows(left, right):
    return lax.dot_general(
        left, right, (((0,), (0,)), ((), ())), preferred_element_type=jnp.float32
    )


def train_pass(grids, labels, down_low, up_low, head, count):
    windows = shifted_windows(grids)
    flat_rows = windows[0].shape[0]
    middle = jnp.zeros((flat_rows, down_low.shape[3]), jnp.float32)
    for offset_index in range(9):
        middle = middle + jnp.dot(
            windows[offset_index],
            down_low[offset_index // 3, offset_index % 3],
            preferred_element_type=jnp.float32,
        )
    active = jax.nn.silu(middle).astype(jnp.bfloat16)
    hidden = grids.reshape(flat_rows, grids.shape[3]).astype(jnp.float32) + jnp.dot(
        active, up_low, preferred_element_type=jnp.float32
    )
    inverse = lax.rsqrt(jnp.mean(hidden * hidden, axis=-1, keepdims=True) + 1e-06)
    normed = hidden * inverse
    head_wide = head.astype(jnp.float32)
    logits = jnp.dot(
        normed, head_wide, precision=lax.Precision.HIGHEST, preferred_element_type=jnp.float32
    )
    flat_labels = labels.reshape(flat_rows)
    living = (flat_labels >= 0).astype(jnp.float32)
    onehot = (flat_labels[:, None] == jnp.arange(head.shape[1], dtype=jnp.int32)[None, :]).astype(
        jnp.float32
    )
    powers = jnp.exp(logits)
    totals = jnp.sum(powers, axis=-1)
    loss_sum = jnp.sum((jnp.log(totals) - jnp.sum(logits * onehot, axis=-1)) * living)
    dlogits = (powers / totals[:, None] - onehot) * living[:, None] / count
    dnormed = lax.dot_general(
        dlogits,
        head_wide,
        (((1,), (1,)), ((), ())),
        precision=lax.Precision.HIGHEST,
        preferred_element_type=jnp.float32,
    )
    dhidden = (
        inverse * (dnormed - normed * jnp.mean(dnormed * normed, axis=-1, keepdims=True))
    ).astype(jnp.bfloat16)
    grad_up = contract_rows(active, dhidden)
    dactive = lax.dot_general(
        dhidden, up_low, (((1,), (1,)), ((), ())), preferred_element_type=jnp.float32
    )
    sigmoid = jax.nn.sigmoid(middle)
    dmiddle = (dactive * sigmoid * (1.0 + middle * (1.0 - sigmoid))).astype(jnp.bfloat16)
    grad_down = jnp.stack([contract_rows(window, dmiddle) for window in windows])
    grad_down = grad_down.reshape(3, 3, grids.shape[3], down_low.shape[3])
    return (loss_sum, grad_down, grad_up)


def step_scale(squares, entries):
    return 0.004 * lax.rsqrt(squares / entries + 1e-06)


def partner_swap(value, pairs):
    return lax.ppermute(value, "ex", perm=pairs)


def stage_pairs(bits_of, peers):
    return [(i, i ^ (1 << bits_of[i % 2])) for i in range(peers)]


def halve_sum(value, axis, bit, pairs, place):
    mine = (place >> bit) & 1
    keep = lax.dynamic_index_in_dim(value, mine, axis, keepdims=False)
    give = lax.dynamic_index_in_dim(value, 1 - mine, axis, keepdims=False)
    return keep + partner_swap(give, pairs)


def double_join(value, axis, bit, pairs, place):
    mine = (place >> bit) & 1
    other = partner_swap(value, pairs)
    first = jnp.where(mine == 0, value, other)
    second = jnp.where(mine == 0, other, value)
    return jnp.stack([first, second], axis=axis)


def swap_bit_axes(value, lead, levels):
    order = list(range(value.ndim))
    order[lead : lead + 4] = [lead + 2, lead + 3, lead, lead + 1]
    return jnp.transpose(value, order)


def shards(feats, targets, task_of, counts, down_w, up_w, head):
    groups = lax.axis_size("task")
    peers = lax.axis_size("ex")
    levels = peers.bit_length() - 1
    sources = feats.shape[0]
    side = feats.shape[1]
    chans = feats.shape[3]
    cells = side * side
    bucket = (2 * sources + groups - 1) // groups
    order = jnp.arange(sources, dtype=jnp.int32)
    earlier = (task_of[:, None] == task_of[None, :]) & (order[None, :] < order[:, None])
    position = jnp.sum(earlier.astype(jnp.int32), axis=1)
    send_feats = (
        jnp.zeros((groups, bucket, side, side, chans), jnp.bfloat16)
        .at[task_of, position]
        .set(feats)
    )
    send_labels = (
        jnp.full((groups, bucket, cells), -1.0, jnp.bfloat16)
        .at[task_of, position]
        .set(targets.astype(jnp.bfloat16))
    )
    come_feats, come_labels = (
        lax.all_to_all(send_feats, "task", split_axis=0, concat_axis=0, tiled=True),
        lax.all_to_all(send_labels, "task", split_axis=0, concat_axis=0, tiled=True),
    )
    held_feats = come_feats.reshape(groups * bucket, side, side, chans)
    held_labels = come_labels.reshape(groups * bucket, cells).astype(jnp.int32)
    count = counts[0].astype(jnp.float32)
    entries = 10.0 * CHANNELS * INNER
    place = lax.axis_index("ex")
    part_chans = down_w.shape[3] // peers
    part_inner = up_w.shape[1] // peers
    inner = down_w.shape[4]
    collected = []
    down_low = down_w[0].astype(jnp.bfloat16)
    upper_low = up_w[0].astype(jnp.bfloat16)
    down_own = lax.dynamic_slice_in_dim(down_w[0], place * part_chans, part_chans, 2)
    up_own = lax.dynamic_slice_in_dim(up_w[0], place * part_inner, part_inner, 0)
    bits_shape = (2,) * levels
    core = place % 2
    second_core = core == 1
    orders = ([0, 1, 2, 3, 4], [0, 3, 4, 1, 2])
    for update_round in range(TRAIN_STEPS):
        loss_sum, grad_down, grad_up = train_pass(
            held_feats, held_labels, down_low, upper_low, head, count
        )
        grad_down = grad_down.reshape((3, 3) + bits_shape + (part_chans, inner))
        grad_up = grad_up.reshape(bits_shape + (part_inner, up_w.shape[2]))
        for stage in range(levels):
            if stage == 1:
                grad_down = jnp.where(second_core, swap_bit_axes(grad_down, 2, levels), grad_down)
                grad_up = jnp.where(second_core, swap_bit_axes(grad_up, 0, levels), grad_up)
            bits_of = (orders[0][stage], orders[1][stage])
            pairs = stage_pairs(bits_of, peers)
            bit = jnp.where(second_core, bits_of[1], bits_of[0])
            grad_down = halve_sum(grad_down, 2 + levels - 1 - stage, bit, pairs, place)
            grad_up = halve_sum(grad_up, levels - 1 - stage, bit, pairs, place)
        squares = jnp.sum(grad_down * grad_down) + jnp.sum(grad_up * grad_up)
        totals = jnp.stack([squares, loss_sum])
        spread = jnp.broadcast_to(totals[None, :], (peers, totals.shape[0]))
        totals = jnp.sum(lax.all_to_all(spread, "ex", 0, 0, tiled=True), axis=0)
        scale = step_scale(totals[0], entries)
        down_own = down_own - scale * grad_down
        up_own = up_own - scale * grad_up
        collected.append(totals[1] / (count * cells))
        if update_round + 1 < TRAIN_STEPS:
            down_low = down_own.astype(jnp.bfloat16)
            upper_low = up_own.astype(jnp.bfloat16)
            for step_index in range(levels):
                stage = levels - 1 - step_index
                if stage == 0:
                    down_low = jnp.where(second_core, swap_bit_axes(down_low, 2, levels), down_low)
                    upper_low = jnp.where(second_core, swap_bit_axes(upper_low, 0, levels), upper_low)
                bits_of = (orders[0][stage], orders[1][stage])
                pairs = stage_pairs(bits_of, peers)
                bit = jnp.where(second_core, bits_of[1], bits_of[0])
                down_low = double_join(down_low, 2 + step_index, bit, pairs, place)
                upper_low = double_join(upper_low, step_index, bit, pairs, place)
            down_low = down_low.reshape(down_w.shape[1:])
            upper_low = upper_low.reshape(up_w.shape[1:])
    return (down_own[None], up_own[None], jnp.stack(collected)[None])


def solution(mesh):
    placed = (
        P(("task", "ex"), None, None, None),
        P(("task", "ex"), None),
        P(("task", "ex")),
        P("task"),
        P("task", None, None, None, None),
        P("task", None, None),
        P(),
    )
    return jax.shard_map(
        shards,
        mesh=mesh,
        in_specs=placed,
        out_specs=(P("task", None, None, "ex", None), P("task", "ex", None), P("task", None)),
        check_vma=False,
    )
```

```python
import jax
import jax.numpy as jnp
from jax import lax
from jax.sharding import PartitionSpec as P

CHANNELS = 512
INNER = 256
TRAIN_STEPS = 2


def shifted_windows(grids):
    count_rows = grids.shape[0]
    side = grids.shape[1]
    padded = jnp.pad(grids, ((0, 0), (1, 1), (1, 1), (0, 0)))
    windows = []
    for offset_index in range(9):
        row_shift = offset_index // 3
        col_shift = offset_index % 3
        window = padded[:, row_shift : row_shift + side, col_shift : col_shift + side, :]
        windows.append(window.reshape(count_rows * side * side, grids.shape[3]))
    return windows


def contract_rows(left, right):
    return lax.dot_general(
        left, right, (((0,), (0,)), ((), ())), preferred_element_type=jnp.float32
    )


def train_pass(grids, labels, down_low, up_low, head, count):
    windows = shifted_windows(grids)
    flat_rows = windows[0].shape[0]
    middle = jnp.zeros((flat_rows, down_low.shape[3]), jnp.float32)
    for offset_index in range(9):
        middle = middle + jnp.dot(
            windows[offset_index],
            down_low[offset_index // 3, offset_index % 3],
            preferred_element_type=jnp.float32,
        )
    active = jax.nn.silu(middle).astype(jnp.bfloat16)
    hidden = grids.reshape(flat_rows, grids.shape[3]).astype(jnp.float32) + jnp.dot(
        active, up_low, preferred_element_type=jnp.float32
    )
    inverse = lax.rsqrt(jnp.mean(hidden * hidden, axis=-1, keepdims=True) + 1e-06)
    normed = hidden * inverse
    head_wide = head.astype(jnp.float32)
    logits = jnp.dot(
        normed, head_wide, precision=lax.Precision.HIGHEST, preferred_element_type=jnp.float32
    )
    flat_labels = labels.reshape(flat_rows)
    living = (flat_labels >= 0).astype(jnp.float32)
    onehot = (flat_labels[:, None] == jnp.arange(head.shape[1], dtype=jnp.int32)[None, :]).astype(
        jnp.float32
    )
    powers = jnp.exp(logits)
    totals = jnp.sum(powers, axis=-1)
    loss_sum = jnp.sum((jnp.log(totals) - jnp.sum(logits * onehot, axis=-1)) * living)
    dlogits = (powers / totals[:, None] - onehot) * living[:, None] / count
    dnormed = lax.dot_general(
        dlogits,
        head_wide,
        (((1,), (1,)), ((), ())),
        precision=lax.Precision.HIGHEST,
        preferred_element_type=jnp.float32,
    )
    dhidden = (
        inverse * (dnormed - normed * jnp.mean(dnormed * normed, axis=-1, keepdims=True))
    ).astype(jnp.bfloat16)
    grad_up = contract_rows(active, dhidden)
    dactive = lax.dot_general(
        dhidden, up_low, (((1,), (1,)), ((), ())), preferred_element_type=jnp.float32
    )
    sigmoid = jax.nn.sigmoid(middle)
    dmiddle = (dactive * sigmoid * (1.0 + middle * (1.0 - sigmoid))).astype(jnp.bfloat16)
    grad_down = jnp.stack([contract_rows(window, dmiddle) for window in windows])
    grad_down = grad_down.reshape(3, 3, grids.shape[3], down_low.shape[3])
    return (loss_sum, grad_down, grad_up)


def step_scale(squares, entries):
    return 0.004 * lax.rsqrt(squares / entries + 1e-06)


EX_AXES = ("z", "y", "core")


def partner_swap(value, pairs):
    return lax.ppermute(value, EX_AXES, perm=pairs)


def stage_pairs(bits_of, peers):
    return [(i, i ^ (1 << bits_of[i % 2])) for i in range(peers)]


def halve_sum(value, axis, bit, pairs, place):
    mine = (place >> bit) & 1
    keep = lax.dynamic_index_in_dim(value, mine, axis, keepdims=False)
    give = lax.dynamic_index_in_dim(value, 1 - mine, axis, keepdims=False)
    return keep + partner_swap(give, pairs)


def double_join(value, axis, bit, pairs, place):
    mine = (place >> bit) & 1
    other = partner_swap(value, pairs)
    first = jnp.where(mine == 0, value, other)
    second = jnp.where(mine == 0, other, value)
    return jnp.stack([first, second], axis=axis)


def swap_bit_axes(value, lead, levels):
    order = list(range(value.ndim))
    order[lead : lead + 4] = [lead + 2, lead + 3, lead, lead + 1]
    return jnp.transpose(value, order)


def shards(feats, targets, task_of, counts, down_w, up_w, head):
    groups = lax.axis_size("task")
    peers = lax.axis_size(EX_AXES)
    levels = peers.bit_length() - 1
    sources = feats.shape[0]
    side = feats.shape[1]
    chans = feats.shape[3]
    cells = side * side
    bucket = (2 * sources + groups - 1) // groups
    order = jnp.arange(sources, dtype=jnp.int32)
    earlier = (task_of[:, None] == task_of[None, :]) & (order[None, :] < order[:, None])
    position = jnp.sum(earlier.astype(jnp.int32), axis=1)
    send_feats = (
        jnp.zeros((groups, bucket, side, side, chans), jnp.bfloat16)
        .at[task_of, position]
        .set(feats)
    )
    send_labels = (
        jnp.full((groups, bucket, cells), -1.0, jnp.bfloat16)
        .at[task_of, position]
        .set(targets.astype(jnp.bfloat16))
    )
    come_feats, come_labels = (
        lax.all_to_all(send_feats, "task", split_axis=0, concat_axis=0, tiled=True),
        lax.all_to_all(send_labels, "task", split_axis=0, concat_axis=0, tiled=True),
    )
    held_feats = come_feats.reshape(groups * bucket, side, side, chans)
    held_labels = come_labels.reshape(groups * bucket, cells).astype(jnp.int32)
    count = counts[0].astype(jnp.float32)
    entries = 10.0 * CHANNELS * INNER
    place = lax.axis_index(EX_AXES)
    part_chans = down_w.shape[3] // peers
    part_inner = up_w.shape[1] // peers
    inner = down_w.shape[4]
    collected = []
    down_low = down_w[0].astype(jnp.bfloat16)
    upper_low = up_w[0].astype(jnp.bfloat16)
    down_own = lax.dynamic_slice_in_dim(down_w[0], place * part_chans, part_chans, 2)
    up_own = lax.dynamic_slice_in_dim(up_w[0], place * part_inner, part_inner, 0)
    core = place % 2
    grid_axes = ("z", "y")
    plane = peers // 2
    core_pairs = [(i, i ^ 1) for i in range(peers)]
    for update_round in range(TRAIN_STEPS):
        loss_sum, grad_down, grad_up = train_pass(
            held_feats, held_labels, down_low, upper_low, head, count
        )
        grad_down = grad_down.reshape(3, 3, plane, 2, part_chans, inner)
        grad_up = grad_up.reshape(plane, 2, part_inner, up_w.shape[2])
        keep_down = lax.dynamic_index_in_dim(grad_down, core, 3, keepdims=False)
        give_down = lax.dynamic_index_in_dim(grad_down, 1 - core, 3, keepdims=False)
        keep_up = lax.dynamic_index_in_dim(grad_up, core, 1, keepdims=False)
        give_up = lax.dynamic_index_in_dim(grad_up, 1 - core, 1, keepdims=False)
        got_down, got_up = lax.ppermute((give_down, give_up), EX_AXES, perm=core_pairs)
        grad_down = keep_down + got_down
        grad_up = keep_up + got_up
        grad_down = jnp.sum(lax.all_to_all(grad_down, grid_axes, 2, 2, tiled=True), axis=2)
        grad_up = jnp.sum(lax.all_to_all(grad_up, grid_axes, 0, 0, tiled=True), axis=0)
        squares = jnp.sum(grad_down * grad_down) + jnp.sum(grad_up * grad_up)
        totals = jnp.stack([squares, loss_sum])
        spread = jnp.broadcast_to(totals[None, :], (peers, totals.shape[0]))
        totals = jnp.sum(lax.all_to_all(spread, EX_AXES, 0, 0, tiled=True), axis=0)
        scale = step_scale(totals[0], entries)
        down_own = down_own - scale * grad_down
        up_own = up_own - scale * grad_up
        collected.append(totals[1] / (count * cells))
        if update_round + 1 < TRAIN_STEPS:
            down_low = down_own.astype(jnp.bfloat16)
            upper_low = up_own.astype(jnp.bfloat16)
            down_low = jnp.broadcast_to(down_low[:, :, None], (3, 3, plane) + down_low.shape[2:])
            upper_low = jnp.broadcast_to(upper_low[None], (plane,) + upper_low.shape)
            down_low = lax.all_to_all(down_low, grid_axes, 2, 2, tiled=True)
            upper_low = lax.all_to_all(upper_low, grid_axes, 0, 0, tiled=True)
            other_down, other_up = lax.ppermute((down_low, upper_low), EX_AXES, perm=core_pairs)
            first_core = core == 0
            down_low = jnp.stack(
                [jnp.where(first_core, down_low, other_down), jnp.where(first_core, other_down, down_low)], axis=3
            )
            upper_low = jnp.stack(
                [jnp.where(first_core, upper_low, other_up), jnp.where(first_core, other_up, upper_low)], axis=1
            )
            down_low = down_low.reshape(down_w.shape[1:])
            upper_low = upper_low.reshape(up_w.shape[1:])
    return (down_own[None], up_own[None], jnp.stack(collected)[None])


def solution(mesh):
    grid = mesh.devices.reshape(mesh.devices.shape[0], 4, -1, 2)
    split_mesh = jax.sharding.Mesh(grid, ("task",) + EX_AXES)
    rows = ("task",) + EX_AXES
    placed = (
        P(rows, None, None, None),
        P(rows, None),
        P(rows),
        P("task"),
        P("task", None, None, None, None),
        P("task", None, None),
        P(),
    )
    return jax.shard_map(
        shards,
        mesh=split_mesh,
        in_specs=placed,
        out_specs=(P("task", None, None, EX_AXES, None), P("task", EX_AXES, None), P("task", None)),
        check_vma=False,
    )
```

```python
import jax
import jax.numpy as jnp
from jax import lax
from jax.sharding import PartitionSpec as P

CHANNELS = 512
INNER = 256
TRAIN_STEPS = 2


def shifted_windows(grids):
    count_rows = grids.shape[0]
    side = grids.shape[1]
    padded = jnp.pad(grids, ((0, 0), (1, 1), (1, 1), (0, 0)))
    windows = []
    for offset_index in range(9):
        row_shift = offset_index // 3
        col_shift = offset_index % 3
        window = padded[:, row_shift : row_shift + side, col_shift : col_shift + side, :]
        windows.append(window.reshape(count_rows * side * side, grids.shape[3]))
    return windows


def contract_rows(left, right):
    return lax.dot_general(
        left, right, (((0,), (0,)), ((), ())), preferred_element_type=jnp.float32
    )


def train_pass(grids, labels, down_low, up_low, head, count):
    windows = shifted_windows(grids)
    flat_rows = windows[0].shape[0]
    middle = jnp.zeros((flat_rows, down_low.shape[3]), jnp.float32)
    for offset_index in range(9):
        middle = middle + jnp.dot(
            windows[offset_index],
            down_low[offset_index // 3, offset_index % 3],
            preferred_element_type=jnp.float32,
        )
    active = jax.nn.silu(middle).astype(jnp.bfloat16)
    hidden = grids.reshape(flat_rows, grids.shape[3]).astype(jnp.float32) + jnp.dot(
        active, up_low, preferred_element_type=jnp.float32
    )
    inverse = lax.rsqrt(jnp.mean(hidden * hidden, axis=-1, keepdims=True) + 1e-06)
    normed = hidden * inverse
    head_wide = head.astype(jnp.float32)
    logits = jnp.dot(
        normed, head_wide, precision=lax.Precision.HIGHEST, preferred_element_type=jnp.float32
    )
    flat_labels = labels.reshape(flat_rows)
    living = (flat_labels >= 0).astype(jnp.float32)
    onehot = (flat_labels[:, None] == jnp.arange(head.shape[1], dtype=jnp.int32)[None, :]).astype(
        jnp.float32
    )
    powers = jnp.exp(logits)
    totals = jnp.sum(powers, axis=-1)
    loss_sum = jnp.sum((jnp.log(totals) - jnp.sum(logits * onehot, axis=-1)) * living)
    dlogits = (powers / totals[:, None] - onehot) * living[:, None] / count
    dnormed = lax.dot_general(
        dlogits,
        head_wide,
        (((1,), (1,)), ((), ())),
        precision=lax.Precision.HIGHEST,
        preferred_element_type=jnp.float32,
    )
    dhidden = (
        inverse * (dnormed - normed * jnp.mean(dnormed * normed, axis=-1, keepdims=True))
    ).astype(jnp.bfloat16)
    grad_up = contract_rows(active, dhidden)
    dactive = lax.dot_general(
        dhidden, up_low, (((1,), (1,)), ((), ())), preferred_element_type=jnp.float32
    )
    sigmoid = jax.nn.sigmoid(middle)
    dmiddle = (dactive * sigmoid * (1.0 + middle * (1.0 - sigmoid))).astype(jnp.bfloat16)
    grad_down = jnp.stack([contract_rows(window, dmiddle) for window in windows], axis=1)
    return (loss_sum, grad_down, grad_up)


def step_scale(squares, entries):
    return 0.004 * lax.rsqrt(squares / entries + 1e-06)


EX_AXES = ("z", "y", "core")


def partner_swap(value, pairs):
    return lax.ppermute(value, EX_AXES, perm=pairs)


def stage_pairs(bits_of, peers):
    return [(i, i ^ (1 << bits_of[i % 2])) for i in range(peers)]


def halve_sum(value, axis, bit, pairs, place):
    mine = (place >> bit) & 1
    keep = lax.dynamic_index_in_dim(value, mine, axis, keepdims=False)
    give = lax.dynamic_index_in_dim(value, 1 - mine, axis, keepdims=False)
    return keep + partner_swap(give, pairs)


def double_join(value, axis, bit, pairs, place):
    mine = (place >> bit) & 1
    other = partner_swap(value, pairs)
    first = jnp.where(mine == 0, value, other)
    second = jnp.where(mine == 0, other, value)
    return jnp.stack([first, second], axis=axis)


def swap_bit_axes(value, lead, levels):
    order = list(range(value.ndim))
    order[lead : lead + 4] = [lead + 2, lead + 3, lead, lead + 1]
    return jnp.transpose(value, order)


def shards(feats, targets, task_of, counts, down_w, up_w, head):
    groups = lax.axis_size("task")
    peers = lax.axis_size(EX_AXES)
    levels = peers.bit_length() - 1
    sources = feats.shape[0]
    side = feats.shape[1]
    chans = feats.shape[3]
    cells = side * side
    bucket = (2 * sources + groups - 1) // groups
    order = jnp.arange(sources, dtype=jnp.int32)
    earlier = (task_of[:, None] == task_of[None, :]) & (order[None, :] < order[:, None])
    position = jnp.sum(earlier.astype(jnp.int32), axis=1)
    send_feats = (
        jnp.zeros((groups, bucket, side, side, chans), jnp.bfloat16)
        .at[task_of, position]
        .set(feats)
    )
    send_labels = (
        jnp.full((groups, bucket, cells), -1.0, jnp.bfloat16)
        .at[task_of, position]
        .set(targets.astype(jnp.bfloat16))
    )
    come_feats, come_labels = (
        lax.all_to_all(send_feats, "task", split_axis=0, concat_axis=0, tiled=True),
        lax.all_to_all(send_labels, "task", split_axis=0, concat_axis=0, tiled=True),
    )
    held_feats = come_feats.reshape(groups * bucket, side, side, chans)
    held_labels = come_labels.reshape(groups * bucket, cells).astype(jnp.int32)
    count = counts[0].astype(jnp.float32)
    entries = 10.0 * CHANNELS * INNER
    place = lax.axis_index(EX_AXES)
    part_chans = down_w.shape[3] // peers
    part_inner = up_w.shape[1] // peers
    inner = down_w.shape[4]
    collected = []
    down_low = down_w[0].astype(jnp.bfloat16)
    upper_low = up_w[0].astype(jnp.bfloat16)
    down_own = lax.dynamic_slice_in_dim(down_w[0], place * part_chans, part_chans, 2)
    up_own = lax.dynamic_slice_in_dim(up_w[0], place * part_inner, part_inner, 0)
    core = place % 2
    grid_axes = ("z", "y")
    plane = peers // 2
    core_pairs = [(i, i ^ 1) for i in range(peers)]
    lanes = 128
    down_span = 9 * part_chans * inner // lanes
    for update_round in range(TRAIN_STEPS):
        loss_sum, grad_down, grad_up = train_pass(
            held_feats, held_labels, down_low, upper_low, head, count
        )
        packed = jnp.concatenate(
            [grad_down.reshape(plane, 2, down_span, lanes), grad_up.reshape(plane, 2, -1, lanes)], axis=2
        )
        keep = lax.dynamic_index_in_dim(packed, core, 1, keepdims=False)
        give = lax.dynamic_index_in_dim(packed, 1 - core, 1, keepdims=False)
        packed = keep + lax.ppermute(give, EX_AXES, perm=core_pairs)
        packed = jnp.sum(lax.all_to_all(packed, grid_axes, 0, 0, tiled=True), axis=0)
        shard_down = packed[:down_span].reshape(part_chans, 3, 3, inner)
        shard_down = jnp.transpose(shard_down, (1, 2, 0, 3))
        shard_up = packed[down_span:].reshape(up_own.shape)
        squares = jnp.sum(shard_down * shard_down) + jnp.sum(shard_up * shard_up)
        totals = jnp.stack([squares, loss_sum])
        spread = jnp.broadcast_to(totals[None, :], (peers, totals.shape[0]))
        totals = jnp.sum(lax.all_to_all(spread, EX_AXES, 0, 0, tiled=True), axis=0)
        scale = step_scale(totals[0], entries)
        down_own = down_own - scale * shard_down
        up_own = up_own - scale * shard_up
        collected.append(totals[1] / (count * cells))
        if update_round + 1 < TRAIN_STEPS:
            low_down = jnp.transpose(down_own.astype(jnp.bfloat16), (2, 0, 1, 3)).reshape(down_span, lanes)
            low_up = up_own.astype(jnp.bfloat16).reshape(-1, lanes)
            block = jnp.concatenate([low_down, low_up], axis=0)
            block = jnp.broadcast_to(block[None], (plane,) + block.shape)
            block = lax.all_to_all(block, grid_axes, 0, 0, tiled=True)
            other = lax.ppermute(block, EX_AXES, perm=core_pairs)
            first_core = core == 0
            block = jnp.stack(
                [jnp.where(first_core, block, other), jnp.where(first_core, other, block)], axis=1
            )
            down_low = block[:, :, :down_span].reshape(down_w.shape[3], 3, 3, inner)
            down_low = jnp.transpose(down_low, (1, 2, 0, 3))
            upper_low = block[:, :, down_span:].reshape(up_w.shape[1:])
    return (down_own[None], up_own[None], jnp.stack(collected)[None])


def solution(mesh):
    grid = mesh.devices.reshape(mesh.devices.shape[0], 4, -1, 2)
    split_mesh = jax.sharding.Mesh(grid, ("task",) + EX_AXES)
    rows = ("task",) + EX_AXES
    placed = (
        P(rows, None, None, None),
        P(rows, None),
        P(rows),
        P("task"),
        P("task", None, None, None, None),
        P("task", None, None),
        P(),
    )
    return jax.shard_map(
        shards,
        mesh=split_mesh,
        in_specs=placed,
        out_specs=(P("task", None, None, EX_AXES, None), P("task", EX_AXES, None), P("task", None)),
        check_vma=False,
    )
```

```python
import jax
import jax.numpy as jnp
from jax import lax
from jax.sharding import PartitionSpec as P

CHANNELS = 512
INNER = 256
TRAIN_STEPS = 2


def shifted_windows(grids):
    count_rows = grids.shape[0]
    side = grids.shape[1]
    padded = jnp.pad(grids, ((0, 0), (1, 1), (1, 1), (0, 0)))
    windows = []
    for offset_index in range(9):
        row_shift = offset_index // 3
        col_shift = offset_index % 3
        window = padded[:, row_shift : row_shift + side, col_shift : col_shift + side, :]
        windows.append(window.reshape(count_rows * side * side, grids.shape[3]))
    return windows


def contract_rows(left, right):
    return lax.dot_general(
        left, right, (((0,), (0,)), ((), ())), preferred_element_type=jnp.float32
    )


def train_pass(grids, labels, down_low, up_low, head, count):
    windows = shifted_windows(grids)
    flat_rows = windows[0].shape[0]
    middle = jnp.zeros((flat_rows, down_low.shape[3]), jnp.float32)
    for offset_index in range(9):
        middle = middle + jnp.dot(
            windows[offset_index],
            down_low[offset_index // 3, offset_index % 3],
            preferred_element_type=jnp.float32,
        )
    active = jax.nn.silu(middle).astype(jnp.bfloat16)
    hidden = grids.reshape(flat_rows, grids.shape[3]).astype(jnp.float32) + jnp.dot(
        active, up_low, preferred_element_type=jnp.float32
    )
    inverse = lax.rsqrt(jnp.mean(hidden * hidden, axis=-1, keepdims=True) + 1e-06)
    normed = hidden * inverse
    head_wide = head.astype(jnp.float32)
    logits = jnp.dot(
        normed, head_wide, precision=lax.Precision.HIGHEST, preferred_element_type=jnp.float32
    )
    flat_labels = labels.reshape(flat_rows)
    living = (flat_labels >= 0).astype(jnp.float32)
    onehot = (flat_labels[:, None] == jnp.arange(head.shape[1], dtype=jnp.int32)[None, :]).astype(
        jnp.float32
    )
    powers = jnp.exp(logits)
    totals = jnp.sum(powers, axis=-1)
    loss_sum = jnp.sum((jnp.log(totals) - jnp.sum(logits * onehot, axis=-1)) * living)
    dlogits = (powers / totals[:, None] - onehot) * living[:, None] / count
    dnormed = lax.dot_general(
        dlogits,
        head_wide,
        (((1,), (1,)), ((), ())),
        precision=lax.Precision.HIGHEST,
        preferred_element_type=jnp.float32,
    )
    dhidden = (
        inverse * (dnormed - normed * jnp.mean(dnormed * normed, axis=-1, keepdims=True))
    ).astype(jnp.bfloat16)
    grad_up = contract_rows(active, dhidden)
    dactive = lax.dot_general(
        dhidden, up_low, (((1,), (1,)), ((), ())), preferred_element_type=jnp.float32
    )
    sigmoid = jax.nn.sigmoid(middle)
    dmiddle = (dactive * sigmoid * (1.0 + middle * (1.0 - sigmoid))).astype(jnp.bfloat16)
    grad_down = jnp.stack([contract_rows(window, dmiddle) for window in windows])
    grad_down = grad_down.reshape(3, 3, grids.shape[3], down_low.shape[3])
    return (loss_sum, grad_down, grad_up)


def step_scale(squares, entries):
    return 0.004 * lax.rsqrt(squares / entries + 1e-06)


def partner_swap(value, pairs):
    return lax.ppermute(value, "ex", perm=pairs)


def stage_pairs(bits_of, peers):
    return [(i, i ^ (1 << bits_of[i % 2])) for i in range(peers)]


def halve_sum(value, axis, bit, pairs, place):
    mine = (place >> bit) & 1
    keep = lax.dynamic_index_in_dim(value, mine, axis, keepdims=False)
    give = lax.dynamic_index_in_dim(value, 1 - mine, axis, keepdims=False)
    sent = partner_swap(give.astype(jnp.bfloat16), pairs)
    return keep + sent.astype(jnp.float32)


def double_join(value, axis, bit, pairs, place):
    mine = (place >> bit) & 1
    other = partner_swap(value, pairs)
    first = jnp.where(mine == 0, value, other)
    second = jnp.where(mine == 0, other, value)
    return jnp.stack([first, second], axis=axis)


def swap_bit_axes(value, lead, levels):
    order = list(range(value.ndim))
    order[lead : lead + 4] = [lead + 2, lead + 3, lead, lead + 1]
    return jnp.transpose(value, order)


def shards(feats, targets, task_of, counts, down_w, up_w, head):
    groups = lax.axis_size("task")
    peers = lax.axis_size("ex")
    levels = peers.bit_length() - 1
    sources = feats.shape[0]
    side = feats.shape[1]
    chans = feats.shape[3]
    cells = side * side
    bucket = (2 * sources + groups - 1) // groups
    order = jnp.arange(sources, dtype=jnp.int32)
    earlier = (task_of[:, None] == task_of[None, :]) & (order[None, :] < order[:, None])
    position = jnp.sum(earlier.astype(jnp.int32), axis=1)
    send_feats = (
        jnp.zeros((groups, bucket, side, side, chans), jnp.bfloat16)
        .at[task_of, position]
        .set(feats)
    )
    send_labels = (
        jnp.full((groups, bucket, cells), -1.0, jnp.bfloat16)
        .at[task_of, position]
        .set(targets.astype(jnp.bfloat16))
    )
    come_feats, come_labels = (
        lax.all_to_all(send_feats, "task", split_axis=0, concat_axis=0, tiled=True),
        lax.all_to_all(send_labels, "task", split_axis=0, concat_axis=0, tiled=True),
    )
    held_feats = come_feats.reshape(groups * bucket, side, side, chans)
    held_labels = come_labels.reshape(groups * bucket, cells).astype(jnp.int32)
    count = counts[0].astype(jnp.float32)
    entries = 10.0 * CHANNELS * INNER
    place = lax.axis_index("ex")
    part_chans = down_w.shape[3] // peers
    part_inner = up_w.shape[1] // peers
    inner = down_w.shape[4]
    collected = []
    down_low = down_w[0].astype(jnp.bfloat16)
    upper_low = up_w[0].astype(jnp.bfloat16)
    down_own = lax.dynamic_slice_in_dim(down_w[0], place * part_chans, part_chans, 2)
    up_own = lax.dynamic_slice_in_dim(up_w[0], place * part_inner, part_inner, 0)
    bits_shape = (2,) * levels
    core = place % 2
    second_core = core == 1
    orders = ([0, 1, 2, 3, 4], [0, 3, 4, 1, 2])
    for update_round in range(TRAIN_STEPS):
        loss_sum, grad_down, grad_up = train_pass(
            held_feats, held_labels, down_low, upper_low, head, count
        )
        grad_down = grad_down.reshape((3, 3) + bits_shape + (part_chans, inner))
        grad_up = grad_up.reshape(bits_shape + (part_inner, up_w.shape[2]))
        for stage in range(levels):
            if stage == 1:
                grad_down = jnp.where(second_core, swap_bit_axes(grad_down, 2, levels), grad_down)
                grad_up = jnp.where(second_core, swap_bit_axes(grad_up, 0, levels), grad_up)
            bits_of = (orders[0][stage], orders[1][stage])
            pairs = stage_pairs(bits_of, peers)
            bit = jnp.where(second_core, bits_of[1], bits_of[0])
            grad_down = halve_sum(grad_down, 2 + levels - 1 - stage, bit, pairs, place)
            grad_up = halve_sum(grad_up, levels - 1 - stage, bit, pairs, place)
        squares = jnp.sum(grad_down * grad_down) + jnp.sum(grad_up * grad_up)
        totals = jnp.stack([squares, loss_sum])
        spread = jnp.broadcast_to(totals[None, :], (peers, totals.shape[0]))
        totals = jnp.sum(lax.all_to_all(spread, "ex", 0, 0, tiled=True), axis=0)
        scale = step_scale(totals[0], entries)
        down_own = down_own - scale * grad_down
        up_own = up_own - scale * grad_up
        collected.append(totals[1] / (count * cells))
        if update_round + 1 < TRAIN_STEPS:
            down_low = down_own.astype(jnp.bfloat16)
            upper_low = up_own.astype(jnp.bfloat16)
            for step_index in range(levels):
                stage = levels - 1 - step_index
                if stage == 0:
                    down_low = jnp.where(second_core, swap_bit_axes(down_low, 2, levels), down_low)
                    upper_low = jnp.where(second_core, swap_bit_axes(upper_low, 0, levels), upper_low)
                bits_of = (orders[0][stage], orders[1][stage])
                pairs = stage_pairs(bits_of, peers)
                bit = jnp.where(second_core, bits_of[1], bits_of[0])
                down_low = double_join(down_low, 2 + step_index, bit, pairs, place)
                upper_low = double_join(upper_low, step_index, bit, pairs, place)
            down_low = down_low.reshape(down_w.shape[1:])
            upper_low = upper_low.reshape(up_w.shape[1:])
    return (down_own[None], up_own[None], jnp.stack(collected)[None])


def solution(mesh):
    placed = (
        P(("task", "ex"), None, None, None),
        P(("task", "ex"), None),
        P(("task", "ex")),
        P("task"),
        P("task", None, None, None, None),
        P("task", None, None),
        P(),
    )
    return jax.shard_map(
        shards,
        mesh=mesh,
        in_specs=placed,
        out_specs=(P("task", None, None, "ex", None), P("task", "ex", None), P("task", None)),
        check_vma=False,
    )
```

```python
import jax
import jax.numpy as jnp
from jax import lax
from jax.sharding import PartitionSpec as P

CHANNELS = 512
INNER = 256
TRAIN_STEPS = 2


def shifted_windows(grids):
    count_rows = grids.shape[0]
    side = grids.shape[1]
    padded = jnp.pad(grids, ((0, 0), (1, 1), (1, 1), (0, 0)))
    windows = []
    for offset_index in range(9):
        row_shift = offset_index // 3
        col_shift = offset_index % 3
        window = padded[:, row_shift : row_shift + side, col_shift : col_shift + side, :]
        windows.append(window.reshape(count_rows * side * side, grids.shape[3]))
    return windows


def contract_rows(left, right):
    return lax.dot_general(
        left, right, (((0,), (0,)), ((), ())), preferred_element_type=jnp.float32
    )


def train_pass(grids, labels, down_low, up_low, head, count):
    windows = shifted_windows(grids)
    flat_rows = windows[0].shape[0]
    middle = jnp.zeros((flat_rows, down_low.shape[3]), jnp.float32)
    for offset_index in range(9):
        middle = middle + jnp.dot(
            windows[offset_index],
            down_low[offset_index // 3, offset_index % 3],
            preferred_element_type=jnp.float32,
        )
    active = jax.nn.silu(middle).astype(jnp.bfloat16)
    hidden = grids.reshape(flat_rows, grids.shape[3]).astype(jnp.float32) + jnp.dot(
        active, up_low, preferred_element_type=jnp.float32
    )
    inverse = lax.rsqrt(jnp.mean(hidden * hidden, axis=-1, keepdims=True) + 1e-06)
    normed = hidden * inverse
    head_wide = head.astype(jnp.float32)
    logits = jnp.dot(
        normed, head_wide, precision=lax.Precision.HIGHEST, preferred_element_type=jnp.float32
    )
    flat_labels = labels.reshape(flat_rows)
    living = (flat_labels >= 0).astype(jnp.float32)
    onehot = (flat_labels[:, None] == jnp.arange(head.shape[1], dtype=jnp.int32)[None, :]).astype(
        jnp.float32
    )
    powers = jnp.exp(logits)
    totals = jnp.sum(powers, axis=-1)
    loss_sum = jnp.sum((jnp.log(totals) - jnp.sum(logits * onehot, axis=-1)) * living)
    dlogits = (powers / totals[:, None] - onehot) * living[:, None] / count
    dnormed = lax.dot_general(
        dlogits,
        head_wide,
        (((1,), (1,)), ((), ())),
        precision=lax.Precision.HIGHEST,
        preferred_element_type=jnp.float32,
    )
    dhidden = (
        inverse * (dnormed - normed * jnp.mean(dnormed * normed, axis=-1, keepdims=True))
    ).astype(jnp.bfloat16)
    grad_up = contract_rows(active, dhidden)
    dactive = lax.dot_general(
        dhidden, up_low, (((1,), (1,)), ((), ())), preferred_element_type=jnp.float32
    )
    sigmoid = jax.nn.sigmoid(middle)
    dmiddle = (dactive * sigmoid * (1.0 + middle * (1.0 - sigmoid))).astype(jnp.bfloat16)
    grad_down = jnp.stack([contract_rows(window, dmiddle) for window in windows])
    grad_down = grad_down.reshape(3, 3, grids.shape[3], down_low.shape[3])
    return (loss_sum, grad_down, grad_up)


def step_scale(squares, entries):
    return 0.004 * lax.rsqrt(squares / entries + 1e-06)


def partner_swap(value, pairs):
    return lax.ppermute(value, "ex", perm=pairs)


def stage_pairs(bits_of, peers):
    return [(i, i ^ (1 << bits_of[i % 2])) for i in range(peers)]


def halve_sum(value, axis, bit, pairs, place):
    mine = (place >> bit) & 1
    keep = lax.dynamic_index_in_dim(value, mine, axis, keepdims=False)
    give = lax.dynamic_index_in_dim(value, 1 - mine, axis, keepdims=False)
    sent = partner_swap(give.astype(jnp.bfloat16), pairs)
    return keep + sent.astype(jnp.float32)


def double_join(value, axis, bit, pairs, place):
    mine = (place >> bit) & 1
    other = partner_swap(value, pairs)
    first = jnp.where(mine == 0, value, other)
    second = jnp.where(mine == 0, other, value)
    return jnp.stack([first, second], axis=axis)


def swap_bit_axes(value, lead, levels):
    order = list(range(value.ndim))
    order[lead : lead + 4] = [lead + 2, lead + 3, lead, lead + 1]
    return jnp.transpose(value, order)


def shards(feats, targets, task_of, counts, down_w, up_w, head):
    groups = lax.axis_size("task")
    peers = lax.axis_size("ex")
    levels = peers.bit_length() - 1
    sources = feats.shape[0]
    side = feats.shape[1]
    chans = feats.shape[3]
    cells = side * side
    bucket = (2 * sources + groups - 1) // groups
    order = jnp.arange(sources, dtype=jnp.int32)
    earlier = (task_of[:, None] == task_of[None, :]) & (order[None, :] < order[:, None])
    position = jnp.sum(earlier.astype(jnp.int32), axis=1)
    send_feats = (
        jnp.zeros((groups, bucket, side, side, chans), jnp.bfloat16)
        .at[task_of, position]
        .set(feats)
    )
    send_labels = (
        jnp.full((groups, bucket, cells), -1.0, jnp.bfloat16)
        .at[task_of, position]
        .set(targets.astype(jnp.bfloat16))
    )
    come_feats, come_labels = (
        lax.all_to_all(send_feats, "task", split_axis=0, concat_axis=0, tiled=True),
        lax.all_to_all(send_labels, "task", split_axis=0, concat_axis=0, tiled=True),
    )
    held_feats = come_feats.reshape(groups * bucket, side, side, chans)
    held_labels = come_labels.reshape(groups * bucket, cells).astype(jnp.int32)
    count = counts[0].astype(jnp.float32)
    entries = 10.0 * CHANNELS * INNER
    place = lax.axis_index("ex")
    part_chans = down_w.shape[3] // peers
    part_inner = up_w.shape[1] // peers
    inner = down_w.shape[4]
    collected = []
    down_low = down_w[0].astype(jnp.bfloat16)
    upper_low = up_w[0].astype(jnp.bfloat16)
    down_own = lax.dynamic_slice_in_dim(down_w[0], place * part_chans, part_chans, 2)
    up_own = lax.dynamic_slice_in_dim(up_w[0], place * part_inner, part_inner, 0)
    bits_shape = (2,) * levels
    core = place % 2
    second_core = core == 1
    orders = ([0, 1, 2, 3, 4], [0, 3, 4, 1, 2])
    for update_round in range(TRAIN_STEPS):
        loss_sum, grad_down, grad_up = train_pass(
            held_feats, held_labels, down_low, upper_low, head, count
        )
        grad_down = grad_down.reshape((3, 3) + bits_shape + (part_chans, inner))
        grad_up = grad_up.reshape(bits_shape + (part_inner, up_w.shape[2]))
        for stage in range(levels):
            if stage == 1:
                grad_down = jnp.where(second_core, swap_bit_axes(grad_down, 2, levels), grad_down)
                grad_up = jnp.where(second_core, swap_bit_axes(grad_up, 0, levels), grad_up)
            bits_of = (orders[0][stage], orders[1][stage])
            pairs = stage_pairs(bits_of, peers)
            bit = jnp.where(second_core, bits_of[1], bits_of[0])
            grad_down = halve_sum(grad_down, 2 + levels - 1 - stage, bit, pairs, place)
            grad_up = halve_sum(grad_up, levels - 1 - stage, bit, pairs, place)
        squares = jnp.sum(grad_down * grad_down) + jnp.sum(grad_up * grad_up)
        totals = jnp.stack([squares, loss_sum])
        spread = jnp.broadcast_to(totals[None, :], (peers, totals.shape[0]))
        totals = jnp.sum(lax.all_to_all(spread, "ex", 0, 0, tiled=True), axis=0)
        scale = step_scale(totals[0], entries)
        down_own = down_own - scale * grad_down
        up_own = up_own - scale * grad_up
        collected.append(totals[1] / (count * cells))
        if update_round + 1 < TRAIN_STEPS:
            down_low = grad_down.astype(jnp.bfloat16)
            upper_low = grad_up.astype(jnp.bfloat16)
            for step_index in range(levels):
                stage = levels - 1 - step_index
                if stage == 0:
                    down_low = jnp.where(second_core, swap_bit_axes(down_low, 2, levels), down_low)
                    upper_low = jnp.where(second_core, swap_bit_axes(upper_low, 0, levels), upper_low)
                bits_of = (orders[0][stage], orders[1][stage])
                pairs = stage_pairs(bits_of, peers)
                bit = jnp.where(second_core, bits_of[1], bits_of[0])
                down_low = double_join(down_low, 2 + step_index, bit, pairs, place)
                upper_low = double_join(upper_low, step_index, bit, pairs, place)
            down_low = down_low.reshape(down_w.shape[1:]).astype(jnp.float32)
            upper_low = upper_low.reshape(up_w.shape[1:]).astype(jnp.float32)
            down_low = (down_w[0] - scale * down_low).astype(jnp.bfloat16)
            upper_low = (up_w[0] - scale * upper_low).astype(jnp.bfloat16)
    return (down_own[None], up_own[None], jnp.stack(collected)[None])


def solution(mesh):
    placed = (
        P(("task", "ex"), None, None, None),
        P(("task", "ex"), None),
        P(("task", "ex")),
        P("task"),
        P("task", None, None, None, None),
        P("task", None, None),
        P(),
    )
    return jax.shard_map(
        shards,
        mesh=mesh,
        in_specs=placed,
        out_specs=(P("task", None, None, "ex", None), P("task", "ex", None), P("task", None)),
        check_vma=False,
    )
```

```python
import jax
import jax.numpy as jnp
from jax import lax
from jax.sharding import PartitionSpec as P

CHANNELS = 512
INNER = 256
TRAIN_STEPS = 2


def shifted_windows(grids):
    count_rows = grids.shape[0]
    side = grids.shape[1]
    padded = jnp.pad(grids, ((0, 0), (1, 1), (1, 1), (0, 0)))
    windows = []
    for offset_index in range(9):
        row_shift = offset_index // 3
        col_shift = offset_index % 3
        window = padded[:, row_shift : row_shift + side, col_shift : col_shift + side, :]
        windows.append(window.reshape(count_rows * side * side, grids.shape[3]))
    return windows


def contract_rows(left, right):
    return lax.dot_general(
        left, right, (((0,), (0,)), ((), ())), preferred_element_type=jnp.float32
    )


def train_pass(grids, labels, down_low, up_low, head, count):
    windows = shifted_windows(grids)
    flat_rows = windows[0].shape[0]
    middle = jnp.zeros((flat_rows, down_low.shape[3]), jnp.float32)
    for offset_index in range(9):
        middle = middle + jnp.dot(
            windows[offset_index],
            down_low[offset_index // 3, offset_index % 3],
            preferred_element_type=jnp.float32,
        )
    active = jax.nn.silu(middle).astype(jnp.bfloat16)
    hidden = grids.reshape(flat_rows, grids.shape[3]).astype(jnp.float32) + jnp.dot(
        active, up_low, preferred_element_type=jnp.float32
    )
    inverse = lax.rsqrt(jnp.mean(hidden * hidden, axis=-1, keepdims=True) + 1e-06)
    normed = hidden * inverse
    head_wide = head.astype(jnp.float32)
    logits = jnp.dot(
        normed, head_wide, precision=lax.Precision.HIGHEST, preferred_element_type=jnp.float32
    )
    flat_labels = labels.reshape(flat_rows)
    living = (flat_labels >= 0).astype(jnp.float32)
    onehot = (flat_labels[:, None] == jnp.arange(head.shape[1], dtype=jnp.int32)[None, :]).astype(
        jnp.float32
    )
    powers = jnp.exp(logits)
    totals = jnp.sum(powers, axis=-1)
    loss_sum = jnp.sum((jnp.log(totals) - jnp.sum(logits * onehot, axis=-1)) * living)
    dlogits = (powers / totals[:, None] - onehot) * living[:, None] / count
    dnormed = lax.dot_general(
        dlogits,
        head_wide,
        (((1,), (1,)), ((), ())),
        precision=lax.Precision.HIGHEST,
        preferred_element_type=jnp.float32,
    )
    dhidden = (
        inverse * (dnormed - normed * jnp.mean(dnormed * normed, axis=-1, keepdims=True))
    ).astype(jnp.bfloat16)
    grad_up = contract_rows(active, dhidden)
    dactive = lax.dot_general(
        dhidden, up_low, (((1,), (1,)), ((), ())), preferred_element_type=jnp.float32
    )
    sigmoid = jax.nn.sigmoid(middle)
    dmiddle = (dactive * sigmoid * (1.0 + middle * (1.0 - sigmoid))).astype(jnp.bfloat16)
    grad_down = jnp.stack([contract_rows(window, dmiddle) for window in windows])
    grad_down = grad_down.reshape(3, 3, grids.shape[3], down_low.shape[3])
    return (loss_sum, grad_down, grad_up)


def step_scale(squares, entries):
    return 0.004 * lax.rsqrt(squares / entries + 1e-06)


def partner_swap(value, pairs):
    return lax.ppermute(value, "ex", perm=pairs)


def stage_pairs(bits_of, peers):
    return [(i, i ^ (1 << bits_of[i % 2])) for i in range(peers)]


def halve_sum(value, axis, bit, pairs, place):
    mine = (place >> bit) & 1
    keep = lax.dynamic_index_in_dim(value, mine, axis, keepdims=False)
    give = lax.dynamic_index_in_dim(value, 1 - mine, axis, keepdims=False)
    sent = partner_swap(give.astype(jnp.bfloat16), pairs)
    return keep + sent.astype(jnp.float32)


def double_join(value, axis, bit, pairs, place):
    mine = (place >> bit) & 1
    other = partner_swap(value, pairs)
    first = jnp.where(mine == 0, value, other)
    second = jnp.where(mine == 0, other, value)
    return jnp.stack([first, second], axis=axis)


def swap_bit_axes(value, lead, levels):
    order = list(range(value.ndim))
    order[lead : lead + 4] = [lead + 2, lead + 3, lead, lead + 1]
    return jnp.transpose(value, order)


def shards(feats, targets, task_of, counts, down_w, up_w, head):
    groups = lax.axis_size("task")
    peers = lax.axis_size("ex")
    levels = peers.bit_length() - 1
    sources = feats.shape[0]
    side = feats.shape[1]
    chans = feats.shape[3]
    cells = side * side
    bucket = (2 * sources + groups - 1) // groups
    order = jnp.arange(sources, dtype=jnp.int32)
    earlier = (task_of[:, None] == task_of[None, :]) & (order[None, :] < order[:, None])
    position = jnp.sum(earlier.astype(jnp.int32), axis=1)
    label_row = jnp.zeros((sources, 1, side, chans), jnp.bfloat16)
    label_row = label_row.at[:, 0, 0, :cells].set(targets.astype(jnp.bfloat16))
    empty_row = jnp.zeros((1, side, chans), jnp.bfloat16).at[0, 0, :cells].set(-1.0)
    send_feats = (
        jnp.broadcast_to(
            jnp.concatenate([jnp.zeros((side, side, chans), jnp.bfloat16), empty_row], axis=0),
            (groups, bucket, side + 1, side, chans),
        )
        .at[task_of, position]
        .set(jnp.concatenate([feats, label_row], axis=1))
    )
    come_feats = lax.all_to_all(send_feats, "task", split_axis=0, concat_axis=0, tiled=True)
    come_feats = come_feats.reshape(groups * bucket, side + 1, side, chans)
    held_feats = come_feats[:, :side]
    held_labels = come_feats[:, side, 0, :cells].astype(jnp.int32)
    count = counts[0].astype(jnp.float32)
    entries = 10.0 * CHANNELS * INNER
    place = lax.axis_index("ex")
    part_chans = down_w.shape[3] // peers
    part_inner = up_w.shape[1] // peers
    inner = down_w.shape[4]
    collected = []
    down_low = down_w[0].astype(jnp.bfloat16)
    upper_low = up_w[0].astype(jnp.bfloat16)
    down_own = lax.dynamic_slice_in_dim(down_w[0], place * part_chans, part_chans, 2)
    up_own = lax.dynamic_slice_in_dim(up_w[0], place * part_inner, part_inner, 0)
    bits_shape = (2,) * levels
    core = place % 2
    second_core = core == 1
    orders = ([0, 1, 2, 3, 4], [0, 3, 4, 1, 2])
    for update_round in range(TRAIN_STEPS):
        loss_sum, grad_down, grad_up = train_pass(
            held_feats, held_labels, down_low, upper_low, head, count
        )
        grad_down = grad_down.reshape((3, 3) + bits_shape + (part_chans, inner))
        grad_up = grad_up.reshape(bits_shape + (part_inner, up_w.shape[2]))
        for stage in range(levels):
            if stage == 1:
                grad_down = jnp.where(second_core, swap_bit_axes(grad_down, 2, levels), grad_down)
                grad_up = jnp.where(second_core, swap_bit_axes(grad_up, 0, levels), grad_up)
            bits_of = (orders[0][stage], orders[1][stage])
            pairs = stage_pairs(bits_of, peers)
            bit = jnp.where(second_core, bits_of[1], bits_of[0])
            grad_down = halve_sum(grad_down, 2 + levels - 1 - stage, bit, pairs, place)
            grad_up = halve_sum(grad_up, levels - 1 - stage, bit, pairs, place)
        squares = jnp.sum(grad_down * grad_down) + jnp.sum(grad_up * grad_up)
        totals = jnp.stack([squares, loss_sum])
        spread = jnp.broadcast_to(totals[None, :], (peers, totals.shape[0]))
        totals = jnp.sum(lax.all_to_all(spread, "ex", 0, 0, tiled=True), axis=0)
        scale = step_scale(totals[0], entries)
        down_own = down_own - scale * grad_down
        up_own = up_own - scale * grad_up
        collected.append(totals[1] / (count * cells))
        if update_round + 1 < TRAIN_STEPS:
            down_low = down_own.astype(jnp.bfloat16)
            upper_low = up_own.astype(jnp.bfloat16)
            for step_index in range(levels):
                stage = levels - 1 - step_index
                if stage == 0:
                    down_low = jnp.where(second_core, swap_bit_axes(down_low, 2, levels), down_low)
                    upper_low = jnp.where(second_core, swap_bit_axes(upper_low, 0, levels), upper_low)
                bits_of = (orders[0][stage], orders[1][stage])
                pairs = stage_pairs(bits_of, peers)
                bit = jnp.where(second_core, bits_of[1], bits_of[0])
                down_low = double_join(down_low, 2 + step_index, bit, pairs, place)
                upper_low = double_join(upper_low, step_index, bit, pairs, place)
            down_low = down_low.reshape(down_w.shape[1:])
            upper_low = upper_low.reshape(up_w.shape[1:])
    return (down_own[None], up_own[None], jnp.stack(collected)[None])


def solution(mesh):
    placed = (
        P(("task", "ex"), None, None, None),
        P(("task", "ex"), None),
        P(("task", "ex")),
        P("task"),
        P("task", None, None, None, None),
        P("task", None, None),
        P(),
    )
    return jax.shard_map(
        shards,
        mesh=mesh,
        in_specs=placed,
        out_specs=(P("task", None, None, "ex", None), P("task", "ex", None), P("task", None)),
        check_vma=False,
    )
```

```python
import jax
import jax.numpy as jnp
from jax import lax
from jax.sharding import PartitionSpec as P

CHANNELS = 512
INNER = 256
TRAIN_STEPS = 2


def shifted_windows(grids):
    count_rows = grids.shape[0]
    side = grids.shape[1]
    padded = jnp.pad(grids, ((0, 0), (1, 1), (1, 1), (0, 0)))
    windows = []
    for offset_index in range(9):
        row_shift = offset_index // 3
        col_shift = offset_index % 3
        window = padded[:, row_shift : row_shift + side, col_shift : col_shift + side, :]
        windows.append(window.reshape(count_rows * side * side, grids.shape[3]))
    return windows


def contract_rows(left, right):
    return lax.dot_general(
        left, right, (((0,), (0,)), ((), ())), preferred_element_type=jnp.float32
    )


def train_pass(grids, labels, down_low, up_low, head, count):
    windows = shifted_windows(grids)
    flat_rows = windows[0].shape[0]
    middle = jnp.zeros((flat_rows, down_low.shape[3]), jnp.float32)
    for offset_index in range(9):
        middle = middle + jnp.dot(
            windows[offset_index],
            down_low[offset_index // 3, offset_index % 3],
            preferred_element_type=jnp.float32,
        )
    active = jax.nn.silu(middle).astype(jnp.bfloat16)
    hidden = grids.reshape(flat_rows, grids.shape[3]).astype(jnp.float32) + jnp.dot(
        active, up_low, preferred_element_type=jnp.float32
    )
    inverse = lax.rsqrt(jnp.mean(hidden * hidden, axis=-1, keepdims=True) + 1e-06)
    normed = hidden * inverse
    head_wide = head.astype(jnp.float32)
    logits = jnp.dot(
        normed, head_wide, precision=lax.Precision.HIGHEST, preferred_element_type=jnp.float32
    )
    flat_labels = labels.reshape(flat_rows)
    living = (flat_labels >= 0).astype(jnp.float32)
    onehot = (flat_labels[:, None] == jnp.arange(head.shape[1], dtype=jnp.int32)[None, :]).astype(
        jnp.float32
    )
    powers = jnp.exp(logits)
    totals = jnp.sum(powers, axis=-1)
    loss_sum = jnp.sum((jnp.log(totals) - jnp.sum(logits * onehot, axis=-1)) * living)
    dlogits = (powers / totals[:, None] - onehot) * living[:, None] / count
    dnormed = lax.dot_general(
        dlogits,
        head_wide,
        (((1,), (1,)), ((), ())),
        precision=lax.Precision.HIGHEST,
        preferred_element_type=jnp.float32,
    )
    dhidden = (
        inverse * (dnormed - normed * jnp.mean(dnormed * normed, axis=-1, keepdims=True))
    ).astype(jnp.bfloat16)
    grad_up = contract_rows(active, dhidden)
    dactive = lax.dot_general(
        dhidden, up_low, (((1,), (1,)), ((), ())), preferred_element_type=jnp.float32
    )
    sigmoid = jax.nn.sigmoid(middle)
    dmiddle = (dactive * sigmoid * (1.0 + middle * (1.0 - sigmoid))).astype(jnp.bfloat16)
    grad_down = jnp.stack([contract_rows(window, dmiddle) for window in windows])
    grad_down = grad_down.reshape(3, 3, grids.shape[3], down_low.shape[3])
    return (loss_sum, grad_down, grad_up)


def step_scale(squares, entries):
    return 0.004 * lax.rsqrt(squares / entries + 1e-06)


def partner_swap(value, pairs):
    return lax.ppermute(value, "ex", perm=pairs)


def stage_pairs(bits_of, peers):
    return [(i, i ^ (1 << bits_of[i % 2])) for i in range(peers)]


def halve_sum(value, axis, bit, pairs, place):
    mine = (place >> bit) & 1
    keep = lax.dynamic_index_in_dim(value, mine, axis, keepdims=False)
    give = lax.dynamic_index_in_dim(value, 1 - mine, axis, keepdims=False)
    sent = partner_swap(give.astype(jnp.bfloat16), pairs)
    return keep + sent.astype(jnp.float32)


def double_join(value, axis, bit, pairs, place):
    mine = (place >> bit) & 1
    other = partner_swap(value, pairs)
    first = jnp.where(mine == 0, value, other)
    second = jnp.where(mine == 0, other, value)
    return jnp.stack([first, second], axis=axis)


def swap_bit_axes(value, lead, levels):
    order = list(range(value.ndim))
    order[lead : lead + 4] = [lead + 2, lead + 3, lead, lead + 1]
    return jnp.transpose(value, order)


def shards(feats, targets, task_of, counts, down_w, up_w, head):
    groups = lax.axis_size("task")
    peers = lax.axis_size("ex")
    levels = peers.bit_length() - 1
    sources = feats.shape[0]
    side = feats.shape[1]
    chans = feats.shape[3]
    cells = side * side
    bucket = (2 * sources + groups - 1) // groups
    order = jnp.arange(sources, dtype=jnp.int32)
    earlier = (task_of[:, None] == task_of[None, :]) & (order[None, :] < order[:, None])
    position = jnp.sum(earlier.astype(jnp.int32), axis=1)
    send_feats = (
        jnp.zeros((groups, bucket, side, side, chans), jnp.bfloat16)
        .at[task_of, position]
        .set(feats)
    )
    send_labels = (
        jnp.full((groups, bucket, cells), -1.0, jnp.bfloat16)
        .at[task_of, position]
        .set(targets.astype(jnp.bfloat16))
    )
    come_feats, come_labels = (
        lax.all_to_all(send_feats, "task", split_axis=0, concat_axis=0, tiled=True),
        lax.all_to_all(send_labels, "task", split_axis=0, concat_axis=0, tiled=True),
    )
    held_feats = come_feats.reshape(groups * bucket, side, side, chans)
    held_labels = come_labels.reshape(groups * bucket, cells).astype(jnp.int32)
    task_place = lax.axis_index("task")
    own_feats = lax.dynamic_index_in_dim(send_feats, task_place, 0, keepdims=False)
    own_labels = lax.dynamic_index_in_dim(send_labels, task_place, 0, keepdims=False).astype(jnp.int32)
    others = [(task_place + shift) % groups for shift in range(1, groups)]
    far_feats = jnp.concatenate(
        [lax.dynamic_index_in_dim(come_feats, source, 0, keepdims=True) for source in others], axis=0
    ).reshape((groups - 1) * bucket, side, side, chans)
    far_labels = jnp.concatenate(
        [lax.dynamic_index_in_dim(come_labels, source, 0, keepdims=True) for source in others], axis=0
    ).reshape((groups - 1) * bucket, cells).astype(jnp.int32)
    count = counts[0].astype(jnp.float32)
    entries = 10.0 * CHANNELS * INNER
    place = lax.axis_index("ex")
    part_chans = down_w.shape[3] // peers
    part_inner = up_w.shape[1] // peers
    inner = down_w.shape[4]
    collected = []
    down_low = down_w[0].astype(jnp.bfloat16)
    upper_low = up_w[0].astype(jnp.bfloat16)
    down_own = lax.dynamic_slice_in_dim(down_w[0], place * part_chans, part_chans, 2)
    up_own = lax.dynamic_slice_in_dim(up_w[0], place * part_inner, part_inner, 0)
    bits_shape = (2,) * levels
    core = place % 2
    second_core = core == 1
    orders = ([0, 1, 2, 3, 4], [0, 3, 4, 1, 2])
    for update_round in range(TRAIN_STEPS):
        if update_round == 0:
            near = train_pass(own_feats, own_labels, down_low, upper_low, head, count)
            far = train_pass(far_feats, far_labels, down_low, upper_low, head, count)
            loss_sum, grad_down, grad_up = [a + b for a, b in zip(near, far)]
        else:
            loss_sum, grad_down, grad_up = train_pass(
                held_feats, held_labels, down_low, upper_low, head, count
            )
        grad_down = grad_down.reshape((3, 3) + bits_shape + (part_chans, inner))
        grad_up = grad_up.reshape(bits_shape + (part_inner, up_w.shape[2]))
        for stage in range(levels):
            if stage == 1:
                grad_down = jnp.where(second_core, swap_bit_axes(grad_down, 2, levels), grad_down)
                grad_up = jnp.where(second_core, swap_bit_axes(grad_up, 0, levels), grad_up)
            bits_of = (orders[0][stage], orders[1][stage])
            pairs = stage_pairs(bits_of, peers)
            bit = jnp.where(second_core, bits_of[1], bits_of[0])
            grad_down = halve_sum(grad_down, 2 + levels - 1 - stage, bit, pairs, place)
            grad_up = halve_sum(grad_up, levels - 1 - stage, bit, pairs, place)
        squares = jnp.sum(grad_down * grad_down) + jnp.sum(grad_up * grad_up)
        totals = jnp.stack([squares, loss_sum])
        spread = jnp.broadcast_to(totals[None, :], (peers, totals.shape[0]))
        totals = jnp.sum(lax.all_to_all(spread, "ex", 0, 0, tiled=True), axis=0)
        scale = step_scale(totals[0], entries)
        down_own = down_own - scale * grad_down
        up_own = up_own - scale * grad_up
        collected.append(totals[1] / (count * cells))
        if update_round + 1 < TRAIN_STEPS:
            down_low = down_own.astype(jnp.bfloat16)
            upper_low = up_own.astype(jnp.bfloat16)
            for step_index in range(levels):
                stage = levels - 1 - step_index
                if stage == 0:
                    down_low = jnp.where(second_core, swap_bit_axes(down_low, 2, levels), down_low)
                    upper_low = jnp.where(second_core, swap_bit_axes(upper_low, 0, levels), upper_low)
                bits_of = (orders[0][stage], orders[1][stage])
                pairs = stage_pairs(bits_of, peers)
                bit = jnp.where(second_core, bits_of[1], bits_of[0])
                down_low = double_join(down_low, 2 + step_index, bit, pairs, place)
                upper_low = double_join(upper_low, step_index, bit, pairs, place)
            down_low = down_low.reshape(down_w.shape[1:])
            upper_low = upper_low.reshape(up_w.shape[1:])
    return (down_own[None], up_own[None], jnp.stack(collected)[None])


def solution(mesh):
    placed = (
        P(("task", "ex"), None, None, None),
        P(("task", "ex"), None),
        P(("task", "ex")),
        P("task"),
        P("task", None, None, None, None),
        P("task", None, None),
        P(),
    )
    return jax.shard_map(
        shards,
        mesh=mesh,
        in_specs=placed,
        out_specs=(P("task", None, None, "ex", None), P("task", "ex", None), P("task", None)),
        check_vma=False,
    )
```

```python
import jax
import jax.numpy as jnp
from jax import lax
from jax.sharding import PartitionSpec as P

CHANNELS = 512
INNER = 256
TRAIN_STEPS = 2


def shifted_windows(grids):
    count_rows = grids.shape[0]
    side = grids.shape[1]
    padded = jnp.pad(grids, ((0, 0), (1, 1), (1, 1), (0, 0)))
    windows = []
    for offset_index in range(9):
        row_shift = offset_index // 3
        col_shift = offset_index % 3
        window = padded[:, row_shift : row_shift + side, col_shift : col_shift + side, :]
        windows.append(window.reshape(count_rows * side * side, grids.shape[3]))
    return windows


def contract_rows(left, right):
    return lax.dot_general(
        left, right, (((0,), (0,)), ((), ())), preferred_element_type=jnp.float32
    )


def train_pass(grids, labels, down_low, up_low, head, count):
    windows = shifted_windows(grids)
    flat_rows = windows[0].shape[0]
    middle = jnp.zeros((flat_rows, down_low.shape[3]), jnp.float32)
    for offset_index in range(9):
        middle = middle + jnp.dot(
            windows[offset_index],
            down_low[offset_index // 3, offset_index % 3],
            preferred_element_type=jnp.float32,
        )
    active = jax.nn.silu(middle).astype(jnp.bfloat16)
    hidden = grids.reshape(flat_rows, grids.shape[3]).astype(jnp.float32) + jnp.dot(
        active, up_low, preferred_element_type=jnp.float32
    )
    inverse = lax.rsqrt(jnp.mean(hidden * hidden, axis=-1, keepdims=True) + 1e-06)
    normed = hidden * inverse
    head_wide = head.astype(jnp.float32)
    logits = jnp.dot(
        normed, head_wide, precision=lax.Precision.HIGHEST, preferred_element_type=jnp.float32
    )
    flat_labels = labels.reshape(flat_rows)
    living = (flat_labels >= 0).astype(jnp.float32)
    onehot = (flat_labels[:, None] == jnp.arange(head.shape[1], dtype=jnp.int32)[None, :]).astype(
        jnp.float32
    )
    powers = jnp.exp(logits)
    totals = jnp.sum(powers, axis=-1)
    loss_sum = jnp.sum((jnp.log(totals) - jnp.sum(logits * onehot, axis=-1)) * living)
    dlogits = (powers / totals[:, None] - onehot) * living[:, None] / count
    dnormed = lax.dot_general(
        dlogits,
        head_wide,
        (((1,), (1,)), ((), ())),
        precision=lax.Precision.HIGHEST,
        preferred_element_type=jnp.float32,
    )
    dhidden = (
        inverse * (dnormed - normed * jnp.mean(dnormed * normed, axis=-1, keepdims=True))
    ).astype(jnp.bfloat16)
    grad_up = contract_rows(active, dhidden)
    dactive = lax.dot_general(
        dhidden, up_low, (((1,), (1,)), ((), ())), preferred_element_type=jnp.float32
    )
    sigmoid = jax.nn.sigmoid(middle)
    dmiddle = (dactive * sigmoid * (1.0 + middle * (1.0 - sigmoid))).astype(jnp.bfloat16)
    grad_down = jnp.stack([contract_rows(window, dmiddle) for window in windows])
    grad_down = grad_down.reshape(3, 3, grids.shape[3], down_low.shape[3])
    return (loss_sum, grad_down, grad_up)


def step_scale(squares, entries):
    return 0.004 * lax.rsqrt(squares / entries + 1e-06)


def partner_swap(value, pairs):
    return lax.ppermute(value, "ex", perm=pairs)


def stage_pairs(bits_of, peers):
    return [(i, i ^ (1 << bits_of[i % 2])) for i in range(peers)]


def halve_sum(value, axis, bit, pairs, place):
    mine = (place >> bit) & 1
    keep = lax.dynamic_index_in_dim(value, mine, axis, keepdims=False)
    give = lax.dynamic_index_in_dim(value, 1 - mine, axis, keepdims=False)
    sent = partner_swap(give.astype(jnp.bfloat16), pairs)
    return keep + sent.astype(jnp.float32)


def double_join(value, axis, bit, pairs, place):
    mine = (place >> bit) & 1
    other = partner_swap(value, pairs)
    first = jnp.where(mine == 0, value, other)
    second = jnp.where(mine == 0, other, value)
    return jnp.stack([first, second], axis=axis)


def swap_bit_axes(value, lead, levels):
    order = list(range(value.ndim))
    order[lead : lead + 4] = [lead + 2, lead + 3, lead, lead + 1]
    return jnp.transpose(value, order)


def shards(feats, targets, task_of, counts, down_w, up_w, head):
    groups = lax.axis_size("task")
    peers = lax.axis_size("ex")
    levels = peers.bit_length() - 1
    sources = feats.shape[0]
    side = feats.shape[1]
    chans = feats.shape[3]
    cells = side * side
    bucket = (2 * sources + groups - 1) // groups
    order = jnp.arange(sources, dtype=jnp.int32)
    earlier = (task_of[:, None] == task_of[None, :]) & (order[None, :] < order[:, None])
    position = jnp.sum(earlier.astype(jnp.int32), axis=1)
    send_feats = (
        jnp.zeros((groups, bucket, side, side, chans), jnp.bfloat16)
        .at[task_of, position]
        .set(feats)
    )
    send_labels = (
        jnp.full((groups, bucket, cells), -1.0, jnp.bfloat16)
        .at[task_of, position]
        .set(targets.astype(jnp.bfloat16))
    )
    come_feats, come_labels = (
        lax.all_to_all(send_feats, "task", split_axis=0, concat_axis=0, tiled=True),
        lax.all_to_all(send_labels, "task", split_axis=0, concat_axis=0, tiled=True),
    )
    held_feats = come_feats.reshape(groups * bucket, side, side, chans)
    held_labels = come_labels.reshape(groups * bucket, cells).astype(jnp.int32)
    count = counts[0].astype(jnp.float32)
    entries = 10.0 * CHANNELS * INNER
    place = lax.axis_index("ex")
    part_chans = down_w.shape[3] // peers
    part_inner = up_w.shape[1] // peers
    inner = down_w.shape[4]
    collected = []
    down_low = down_w[0].astype(jnp.bfloat16)
    upper_low = up_w[0].astype(jnp.bfloat16)
    down_own = lax.dynamic_slice_in_dim(down_w[0], place * part_chans, part_chans, 2)
    up_own = lax.dynamic_slice_in_dim(up_w[0], place * part_inner, part_inner, 0)
    bits_shape = (2,) * levels
    core = place % 2
    second_core = core == 1
    orders = ([0, 1, 2, 3, 4], [0, 3, 4, 1, 2])
    for update_round in range(TRAIN_STEPS):
        loss_sum, grad_down, grad_up = train_pass(
            held_feats, held_labels, down_low, upper_low, head, count
        )
        grad_down = grad_down.reshape((3, 3) + bits_shape + (part_chans, inner))
        grad_up = grad_up.reshape(peers, part_inner, up_w.shape[2]).astype(jnp.bfloat16)
        grad_up = lax.all_to_all(grad_up, "ex", 0, 0, tiled=True)
        grad_up = jnp.sum(grad_up.astype(jnp.float32), axis=0)
        for stage in range(levels):
            if stage == 1:
                grad_down = jnp.where(second_core, swap_bit_axes(grad_down, 2, levels), grad_down)
            bits_of = (orders[0][stage], orders[1][stage])
            pairs = stage_pairs(bits_of, peers)
            bit = jnp.where(second_core, bits_of[1], bits_of[0])
            grad_down = halve_sum(grad_down, 2 + levels - 1 - stage, bit, pairs, place)
        squares = jnp.sum(grad_down * grad_down) + jnp.sum(grad_up * grad_up)
        totals = jnp.stack([squares, loss_sum])
        spread = jnp.broadcast_to(totals[None, :], (peers, totals.shape[0]))
        totals = jnp.sum(lax.all_to_all(spread, "ex", 0, 0, tiled=True), axis=0)
        scale = step_scale(totals[0], entries)
        down_own = down_own - scale * grad_down
        up_own = up_own - scale * grad_up
        collected.append(totals[1] / (count * cells))
        if update_round + 1 < TRAIN_STEPS:
            down_low = down_own.astype(jnp.bfloat16)
            upper_low = up_own.astype(jnp.bfloat16)
            upper_low = jnp.broadcast_to(upper_low[None], (peers,) + upper_low.shape)
            upper_low = lax.all_to_all(upper_low, "ex", 0, 0, tiled=True)
            for step_index in range(levels):
                stage = levels - 1 - step_index
                if stage == 0:
                    down_low = jnp.where(second_core, swap_bit_axes(down_low, 2, levels), down_low)
                bits_of = (orders[0][stage], orders[1][stage])
                pairs = stage_pairs(bits_of, peers)
                bit = jnp.where(second_core, bits_of[1], bits_of[0])
                down_low = double_join(down_low, 2 + step_index, bit, pairs, place)
            down_low = down_low.reshape(down_w.shape[1:])
            upper_low = upper_low.reshape(up_w.shape[1:])
    return (down_own[None], up_own[None], jnp.stack(collected)[None])


def solution(mesh):
    placed = (
        P(("task", "ex"), None, None, None),
        P(("task", "ex"), None),
        P(("task", "ex")),
        P("task"),
        P("task", None, None, None, None),
        P("task", None, None),
        P(),
    )
    return jax.shard_map(
        shards,
        mesh=mesh,
        in_specs=placed,
        out_specs=(P("task", None, None, "ex", None), P("task", "ex", None), P("task", None)),
        check_vma=False,
    )
```

```python
import jax
import jax.numpy as jnp
from jax import lax
from jax.sharding import PartitionSpec as P

CHANNELS = 512
INNER = 256
TRAIN_STEPS = 2


def shifted_windows(grids):
    count_rows = grids.shape[0]
    side = grids.shape[1]
    padded = jnp.pad(grids, ((0, 0), (1, 1), (1, 1), (0, 0)))
    windows = []
    for offset_index in range(9):
        row_shift = offset_index // 3
        col_shift = offset_index % 3
        window = padded[:, row_shift : row_shift + side, col_shift : col_shift + side, :]
        windows.append(window.reshape(count_rows * side * side, grids.shape[3]))
    return windows


def contract_rows(left, right):
    return lax.dot_general(
        left, right, (((0,), (0,)), ((), ())), preferred_element_type=jnp.float32
    )


def train_pass(grids, labels, down_low, up_low, head, count):
    windows = shifted_windows(grids)
    flat_rows = windows[0].shape[0]
    middle = jnp.zeros((flat_rows, down_low.shape[3]), jnp.float32)
    for offset_index in range(9):
        middle = middle + jnp.dot(
            windows[offset_index],
            down_low[offset_index // 3, offset_index % 3],
            preferred_element_type=jnp.float32,
        )
    active = jax.nn.silu(middle).astype(jnp.bfloat16)
    hidden = grids.reshape(flat_rows, grids.shape[3]).astype(jnp.float32) + jnp.dot(
        active, up_low, preferred_element_type=jnp.float32
    )
    inverse = lax.rsqrt(jnp.mean(hidden * hidden, axis=-1, keepdims=True) + 1e-06)
    normed = hidden * inverse
    head_wide = head.astype(jnp.float32)
    logits = jnp.dot(
        normed, head_wide, precision=lax.Precision.HIGHEST, preferred_element_type=jnp.float32
    )
    flat_labels = labels.reshape(flat_rows)
    living = (flat_labels >= 0).astype(jnp.float32)
    onehot = (flat_labels[:, None] == jnp.arange(head.shape[1], dtype=jnp.int32)[None, :]).astype(
        jnp.float32
    )
    powers = jnp.exp(logits)
    totals = jnp.sum(powers, axis=-1)
    loss_sum = jnp.sum((jnp.log(totals) - jnp.sum(logits * onehot, axis=-1)) * living)
    dlogits = (powers / totals[:, None] - onehot) * living[:, None] / count
    dnormed = lax.dot_general(
        dlogits,
        head_wide,
        (((1,), (1,)), ((), ())),
        precision=lax.Precision.HIGHEST,
        preferred_element_type=jnp.float32,
    )
    dhidden = (
        inverse * (dnormed - normed * jnp.mean(dnormed * normed, axis=-1, keepdims=True))
    ).astype(jnp.bfloat16)
    grad_up = contract_rows(active, dhidden)
    dactive = lax.dot_general(
        dhidden, up_low, (((1,), (1,)), ((), ())), preferred_element_type=jnp.float32
    )
    sigmoid = jax.nn.sigmoid(middle)
    dmiddle = (dactive * sigmoid * (1.0 + middle * (1.0 - sigmoid))).astype(jnp.bfloat16)
    grad_down = jnp.stack([contract_rows(window, dmiddle) for window in windows])
    grad_down = grad_down.reshape(3, 3, grids.shape[3], down_low.shape[3])
    return (loss_sum, grad_down, grad_up)


def step_scale(squares, entries):
    return 0.004 * lax.rsqrt(squares / entries + 1e-06)


def partner_swap(value, pairs):
    return lax.ppermute(value, "ex", perm=pairs)


STAGE_MASKS = (1, 2, 6, 8, 24)


def stage_pairs(bits_of, peers):
    return [(i, i ^ STAGE_MASKS[bits_of[i % 2]]) for i in range(peers)]


def stage_side(bit, place):
    if bit in (1, 3):
        return ((place >> bit) ^ (place >> (bit + 1))) & 1
    return (place >> bit) & 1


def gray_rows(value, lead):
    for high in (lead, lead + 2):
        low_half = lax.index_in_dim(value, 0, high, keepdims=True)
        high_half = jnp.flip(lax.index_in_dim(value, 1, high, keepdims=True), axis=high + 1)
        value = jnp.concatenate([low_half, high_half], axis=high)
    return value


def halve_sum(value, axis, mine, pairs, place):
    keep = lax.dynamic_index_in_dim(value, mine, axis, keepdims=False)
    give = lax.dynamic_index_in_dim(value, 1 - mine, axis, keepdims=False)
    sent = partner_swap(give.astype(jnp.bfloat16), pairs)
    return keep + sent.astype(jnp.float32)


def double_join(value, axis, mine, pairs, place):
    other = partner_swap(value, pairs)
    first = jnp.where(mine == 0, value, other)
    second = jnp.where(mine == 0, other, value)
    return jnp.stack([first, second], axis=axis)


def swap_bit_axes(value, lead, levels):
    order = list(range(value.ndim))
    order[lead : lead + 4] = [lead + 2, lead + 3, lead, lead + 1]
    return jnp.transpose(value, order)


def shards(feats, targets, task_of, counts, down_w, up_w, head):
    groups = lax.axis_size("task")
    peers = lax.axis_size("ex")
    levels = peers.bit_length() - 1
    sources = feats.shape[0]
    side = feats.shape[1]
    chans = feats.shape[3]
    cells = side * side
    bucket = (2 * sources + groups - 1) // groups
    order = jnp.arange(sources, dtype=jnp.int32)
    earlier = (task_of[:, None] == task_of[None, :]) & (order[None, :] < order[:, None])
    position = jnp.sum(earlier.astype(jnp.int32), axis=1)
    send_feats = (
        jnp.zeros((groups, bucket, side, side, chans), jnp.bfloat16)
        .at[task_of, position]
        .set(feats)
    )
    send_labels = (
        jnp.full((groups, bucket, cells), -1.0, jnp.bfloat16)
        .at[task_of, position]
        .set(targets.astype(jnp.bfloat16))
    )
    come_feats, come_labels = (
        lax.all_to_all(send_feats, "task", split_axis=0, concat_axis=0, tiled=True),
        lax.all_to_all(send_labels, "task", split_axis=0, concat_axis=0, tiled=True),
    )
    held_feats = come_feats.reshape(groups * bucket, side, side, chans)
    held_labels = come_labels.reshape(groups * bucket, cells).astype(jnp.int32)
    count = counts[0].astype(jnp.float32)
    entries = 10.0 * CHANNELS * INNER
    place = lax.axis_index("ex")
    part_chans = down_w.shape[3] // peers
    part_inner = up_w.shape[1] // peers
    inner = down_w.shape[4]
    collected = []
    down_low = down_w[0].astype(jnp.bfloat16)
    upper_low = up_w[0].astype(jnp.bfloat16)
    down_own = lax.dynamic_slice_in_dim(down_w[0], place * part_chans, part_chans, 2)
    up_own = lax.dynamic_slice_in_dim(up_w[0], place * part_inner, part_inner, 0)
    bits_shape = (2,) * levels
    core = place % 2
    second_core = core == 1
    orders = ([0, 1, 2, 3, 4], [0, 3, 4, 1, 2])
    for update_round in range(TRAIN_STEPS):
        loss_sum, grad_down, grad_up = train_pass(
            held_feats, held_labels, down_low, upper_low, head, count
        )
        grad_down = grad_down.reshape((3, 3) + bits_shape + (part_chans, inner))
        grad_up = grad_up.reshape(bits_shape + (part_inner, up_w.shape[2]))
        for stage in range(levels):
            if stage == 1:
                grad_down = gray_rows(grad_down, 2)
                grad_up = gray_rows(grad_up, 0)
                grad_down = jnp.where(second_core, swap_bit_axes(grad_down, 2, levels), grad_down)
                grad_up = jnp.where(second_core, swap_bit_axes(grad_up, 0, levels), grad_up)
            bits_of = (orders[0][stage], orders[1][stage])
            pairs = stage_pairs(bits_of, peers)
            bit = jnp.where(second_core, stage_side(bits_of[1], place), stage_side(bits_of[0], place))
            grad_down = halve_sum(grad_down, 2 + levels - 1 - stage, bit, pairs, place)
            grad_up = halve_sum(grad_up, levels - 1 - stage, bit, pairs, place)
        squares = jnp.sum(grad_down * grad_down) + jnp.sum(grad_up * grad_up)
        totals = jnp.stack([squares, loss_sum])
        spread = jnp.broadcast_to(totals[None, :], (peers, totals.shape[0]))
        totals = jnp.sum(lax.all_to_all(spread, "ex", 0, 0, tiled=True), axis=0)
        scale = step_scale(totals[0], entries)
        down_own = down_own - scale * grad_down
        up_own = up_own - scale * grad_up
        collected.append(totals[1] / (count * cells))
        if update_round + 1 < TRAIN_STEPS:
            down_low = down_own.astype(jnp.bfloat16)
            upper_low = up_own.astype(jnp.bfloat16)
            for step_index in range(levels):
                stage = levels - 1 - step_index
                if stage == 0:
                    down_low = jnp.where(second_core, swap_bit_axes(down_low, 2, levels), down_low)
                    upper_low = jnp.where(second_core, swap_bit_axes(upper_low, 0, levels), upper_low)
                    down_low = gray_rows(down_low, 2)
                    upper_low = gray_rows(upper_low, 0)
                bits_of = (orders[0][stage], orders[1][stage])
                pairs = stage_pairs(bits_of, peers)
                bit = jnp.where(second_core, stage_side(bits_of[1], place), stage_side(bits_of[0], place))
                down_low = double_join(down_low, 2 + step_index, bit, pairs, place)
                upper_low = double_join(upper_low, step_index, bit, pairs, place)
            down_low = down_low.reshape(down_w.shape[1:])
            upper_low = upper_low.reshape(up_w.shape[1:])
    return (down_own[None], up_own[None], jnp.stack(collected)[None])


def solution(mesh):
    placed = (
        P(("task", "ex"), None, None, None),
        P(("task", "ex"), None),
        P(("task", "ex")),
        P("task"),
        P("task", None, None, None, None),
        P("task", None, None),
        P(),
    )
    return jax.shard_map(
        shards,
        mesh=mesh,
        in_specs=placed,
        out_specs=(P("task", None, None, "ex", None), P("task", "ex", None), P("task", None)),
        check_vma=False,
    )
```

```python
import jax
import jax.numpy as jnp
from jax import lax
from jax.sharding import PartitionSpec as P

CHANNELS = 512
INNER = 256
TRAIN_STEPS = 2


def shifted_windows(grids):
    count_rows = grids.shape[0]
    side = grids.shape[1]
    padded = jnp.pad(grids, ((0, 0), (1, 1), (1, 1), (0, 0)))
    windows = []
    for offset_index in range(9):
        row_shift = offset_index // 3
        col_shift = offset_index % 3
        window = padded[:, row_shift : row_shift + side, col_shift : col_shift + side, :]
        windows.append(window.reshape(count_rows * side * side, grids.shape[3]))
    return windows


def contract_rows(left, right):
    return lax.dot_general(
        left, right, (((0,), (0,)), ((), ())), preferred_element_type=jnp.float32
    )


def train_pass(grids, labels, down_low, up_low, head, count):
    windows = shifted_windows(grids)
    flat_rows = windows[0].shape[0]
    middle = jnp.zeros((flat_rows, down_low.shape[3]), jnp.float32)
    for offset_index in range(9):
        middle = middle + jnp.dot(
            windows[offset_index],
            down_low[offset_index // 3, offset_index % 3],
            preferred_element_type=jnp.float32,
        )
    active = jax.nn.silu(middle).astype(jnp.bfloat16)
    hidden = grids.reshape(flat_rows, grids.shape[3]).astype(jnp.float32) + jnp.dot(
        active, up_low, preferred_element_type=jnp.float32
    )
    inverse = lax.rsqrt(jnp.mean(hidden * hidden, axis=-1, keepdims=True) + 1e-06)
    normed = hidden * inverse
    head_wide = head.astype(jnp.float32)
    logits = jnp.dot(
        normed, head_wide, precision=lax.Precision.HIGHEST, preferred_element_type=jnp.float32
    )
    flat_labels = labels.reshape(flat_rows)
    living = (flat_labels >= 0).astype(jnp.float32)
    onehot = (flat_labels[:, None] == jnp.arange(head.shape[1], dtype=jnp.int32)[None, :]).astype(
        jnp.float32
    )
    powers = jnp.exp(logits)
    totals = jnp.sum(powers, axis=-1)
    loss_sum = jnp.sum((jnp.log(totals) - jnp.sum(logits * onehot, axis=-1)) * living)
    dlogits = (powers / totals[:, None] - onehot) * living[:, None] / count
    dnormed = lax.dot_general(
        dlogits,
        head_wide,
        (((1,), (1,)), ((), ())),
        precision=lax.Precision.HIGHEST,
        preferred_element_type=jnp.float32,
    )
    dhidden = (
        inverse * (dnormed - normed * jnp.mean(dnormed * normed, axis=-1, keepdims=True))
    ).astype(jnp.bfloat16)
    grad_up = contract_rows(active, dhidden)
    dactive = lax.dot_general(
        dhidden, up_low, (((1,), (1,)), ((), ())), preferred_element_type=jnp.float32
    )
    sigmoid = jax.nn.sigmoid(middle)
    dmiddle = (dactive * sigmoid * (1.0 + middle * (1.0 - sigmoid))).astype(jnp.bfloat16)
    grad_down = jnp.stack([contract_rows(window, dmiddle) for window in windows])
    grad_down = grad_down.reshape(3, 3, grids.shape[3], down_low.shape[3])
    return (loss_sum, grad_down, grad_up)


def step_scale(squares, entries):
    return 0.004 * lax.rsqrt(squares / entries + 1e-06)


def partner_swap(value, pairs):
    return lax.ppermute(value, "ex", perm=pairs)


def stage_pairs(bits_of, peers):
    return [(i, i ^ (1 << bits_of[i % 2])) for i in range(peers)]


def halve_sum(value, axis, bit, pairs, place):
    mine = (place >> bit) & 1
    keep = lax.dynamic_index_in_dim(value, mine, axis, keepdims=False)
    give = lax.dynamic_index_in_dim(value, 1 - mine, axis, keepdims=False)
    sent = partner_swap(give.astype(jnp.bfloat16), pairs)
    return keep + sent.astype(jnp.float32)


def double_join(value, axis, bit, pairs, place):
    mine = (place >> bit) & 1
    other = partner_swap(value, pairs)
    first = jnp.where(mine == 0, value, other)
    second = jnp.where(mine == 0, other, value)
    return jnp.stack([first, second], axis=axis)


def swap_bit_axes(value, lead, levels):
    order = list(range(value.ndim))
    order[lead : lead + 4] = [lead + 2, lead + 3, lead, lead + 1]
    return jnp.transpose(value, order)


def shards(feats, targets, task_of, counts, down_w, up_w, head):
    groups = lax.axis_size("task")
    peers = lax.axis_size("ex")
    levels = peers.bit_length() - 1
    sources = feats.shape[0]
    side = feats.shape[1]
    chans = feats.shape[3]
    cells = side * side
    bucket = (2 * sources + groups - 1) // groups
    order = jnp.arange(sources, dtype=jnp.int32)
    earlier = (task_of[:, None] == task_of[None, :]) & (order[None, :] < order[:, None])
    position = jnp.sum(earlier.astype(jnp.int32), axis=1)
    send_feats = (
        jnp.zeros((groups, bucket, side, side, chans), jnp.bfloat16)
        .at[task_of, position]
        .set(feats)
    )
    send_labels = (
        jnp.full((groups, bucket, cells), -1.0, jnp.bfloat16)
        .at[task_of, position]
        .set(targets.astype(jnp.bfloat16))
    )
    come_feats, come_labels = (
        lax.all_to_all(send_feats, "task", split_axis=0, concat_axis=0, tiled=True),
        lax.all_to_all(send_labels, "task", split_axis=0, concat_axis=0, tiled=True),
    )
    held_feats = come_feats.reshape(groups * bucket, side, side, chans)
    held_labels = come_labels.reshape(groups * bucket, cells).astype(jnp.int32)
    count = counts[0].astype(jnp.float32)
    entries = 10.0 * CHANNELS * INNER
    place = lax.axis_index("ex")
    part_chans = down_w.shape[3] // peers
    part_inner = up_w.shape[1] // peers
    inner = down_w.shape[4]
    collected = []
    down_low = down_w[0].astype(jnp.bfloat16)
    upper_low = up_w[0].astype(jnp.bfloat16)
    down_own = lax.dynamic_slice_in_dim(down_w[0], place * part_chans, part_chans, 2)
    up_own = lax.dynamic_slice_in_dim(up_w[0], place * part_inner, part_inner, 0)
    bits_shape = (2,) * levels
    core = place % 2
    second_core = core == 1
    orders = ([0, 1, 2, 3, 4], [0, 3, 4, 1, 2])
    for update_round in range(TRAIN_STEPS):
        loss_sum, grad_down, grad_up = train_pass(
            held_feats, held_labels, down_low, upper_low, head, count
        )
        grad_down = grad_down.reshape((3, 3) + bits_shape + (part_chans, inner))
        grad_up = grad_up.reshape(bits_shape + (part_inner, up_w.shape[2]))
        for stage in range(levels):
            if stage == 1:
                grad_down = lax.cond(second_core, lambda v: swap_bit_axes(v, 2, levels), lambda v: v, grad_down)
                grad_up = lax.cond(second_core, lambda v: swap_bit_axes(v, 0, levels), lambda v: v, grad_up)
            bits_of = (orders[0][stage], orders[1][stage])
            pairs = stage_pairs(bits_of, peers)
            bit = jnp.where(second_core, bits_of[1], bits_of[0])
            grad_down = halve_sum(grad_down, 2 + levels - 1 - stage, bit, pairs, place)
            grad_up = halve_sum(grad_up, levels - 1 - stage, bit, pairs, place)
        squares = jnp.sum(grad_down * grad_down) + jnp.sum(grad_up * grad_up)
        totals = jnp.stack([squares, loss_sum])
        spread = jnp.broadcast_to(totals[None, :], (peers, totals.shape[0]))
        totals = jnp.sum(lax.all_to_all(spread, "ex", 0, 0, tiled=True), axis=0)
        scale = step_scale(totals[0], entries)
        down_own = down_own - scale * grad_down
        up_own = up_own - scale * grad_up
        collected.append(totals[1] / (count * cells))
        if update_round + 1 < TRAIN_STEPS:
            down_low = down_own.astype(jnp.bfloat16)
            upper_low = up_own.astype(jnp.bfloat16)
            for step_index in range(levels):
                stage = levels - 1 - step_index
                if stage == 0:
                    down_low = lax.cond(second_core, lambda v: swap_bit_axes(v, 2, levels), lambda v: v, down_low)
                    upper_low = lax.cond(second_core, lambda v: swap_bit_axes(v, 0, levels), lambda v: v, upper_low)
                bits_of = (orders[0][stage], orders[1][stage])
                pairs = stage_pairs(bits_of, peers)
                bit = jnp.where(second_core, bits_of[1], bits_of[0])
                down_low = double_join(down_low, 2 + step_index, bit, pairs, place)
                upper_low = double_join(upper_low, step_index, bit, pairs, place)
            down_low = down_low.reshape(down_w.shape[1:])
            upper_low = upper_low.reshape(up_w.shape[1:])
    return (down_own[None], up_own[None], jnp.stack(collected)[None])


def solution(mesh):
    placed = (
        P(("task", "ex"), None, None, None),
        P(("task", "ex"), None),
        P(("task", "ex")),
        P("task"),
        P("task", None, None, None, None),
        P("task", None, None),
        P(),
    )
    return jax.shard_map(
        shards,
        mesh=mesh,
        in_specs=placed,
        out_specs=(P("task", None, None, "ex", None), P("task", "ex", None), P("task", None)),
        check_vma=False,
    )
```

```python
import jax
import jax.numpy as jnp
from jax import lax
from jax.sharding import PartitionSpec as P

CHANNELS = 512
INNER = 256
TRAIN_STEPS = 2


def shifted_windows(grids):
    count_rows = grids.shape[0]
    side = grids.shape[1]
    padded = jnp.pad(grids, ((0, 0), (1, 1), (1, 1), (0, 0)))
    windows = []
    for offset_index in range(9):
        row_shift = offset_index // 3
        col_shift = offset_index % 3
        window = padded[:, row_shift : row_shift + side, col_shift : col_shift + side, :]
        windows.append(window.reshape(count_rows * side * side, grids.shape[3]))
    return windows


def contract_rows(left, right):
    return lax.dot_general(
        left, right, (((0,), (0,)), ((), ())), preferred_element_type=jnp.float32
    )


def train_pass(grids, labels, down_low, up_low, head, count):
    windows = shifted_windows(grids)
    flat_rows = windows[0].shape[0]
    middle = jnp.zeros((flat_rows, down_low.shape[3]), jnp.float32)
    for offset_index in range(9):
        middle = middle + jnp.dot(
            windows[offset_index],
            down_low[offset_index // 3, offset_index % 3],
            preferred_element_type=jnp.float32,
        )
    active = jax.nn.silu(middle).astype(jnp.bfloat16)
    hidden = grids.reshape(flat_rows, grids.shape[3]).astype(jnp.float32) + jnp.dot(
        active, up_low, preferred_element_type=jnp.float32
    )
    inverse = lax.rsqrt(jnp.mean(hidden * hidden, axis=-1, keepdims=True) + 1e-06)
    normed = hidden * inverse
    head_wide = head.astype(jnp.float32)
    logits = jnp.dot(
        normed, head_wide, precision=lax.Precision.HIGHEST, preferred_element_type=jnp.float32
    )
    flat_labels = labels.reshape(flat_rows)
    living = (flat_labels >= 0).astype(jnp.float32)
    onehot = (flat_labels[:, None] == jnp.arange(head.shape[1], dtype=jnp.int32)[None, :]).astype(
        jnp.float32
    )
    powers = jnp.exp(logits)
    totals = jnp.sum(powers, axis=-1)
    loss_sum = jnp.sum((jnp.log(totals) - jnp.sum(logits * onehot, axis=-1)) * living)
    dlogits = (powers / totals[:, None] - onehot) * living[:, None] / count
    dnormed = lax.dot_general(
        dlogits,
        head_wide,
        (((1,), (1,)), ((), ())),
        precision=lax.Precision.HIGHEST,
        preferred_element_type=jnp.float32,
    )
    dhidden = (
        inverse * (dnormed - normed * jnp.mean(dnormed * normed, axis=-1, keepdims=True))
    ).astype(jnp.bfloat16)
    grad_up = contract_rows(active, dhidden)
    dactive = lax.dot_general(
        dhidden, up_low, (((1,), (1,)), ((), ())), preferred_element_type=jnp.float32
    )
    sigmoid = jax.nn.sigmoid(middle)
    dmiddle = (dactive * sigmoid * (1.0 + middle * (1.0 - sigmoid))).astype(jnp.bfloat16)
    grad_down = jnp.stack([contract_rows(window, dmiddle) for window in windows])
    grad_down = grad_down.reshape(3, 3, grids.shape[3], down_low.shape[3])
    return (loss_sum, grad_down, grad_up)


def step_scale(squares, entries):
    return 0.004 * lax.rsqrt(squares / entries + 1e-06)


def partner_swap(value, pairs):
    return lax.ppermute(value, "ex", perm=pairs)


def stage_pairs(bits_of, peers):
    return [(i, i ^ (1 << bits_of[i % 2])) for i in range(peers)]


def halve_sum(value, axis, bit, pairs, place):
    mine = (place >> bit) & 1
    keep = lax.dynamic_index_in_dim(value, mine, axis, keepdims=False)
    give = lax.dynamic_index_in_dim(value, 1 - mine, axis, keepdims=False)
    sent = partner_swap(give.astype(jnp.bfloat16), pairs)
    return keep + sent.astype(jnp.float32)


def double_join(value, axis, bit, pairs, place):
    mine = (place >> bit) & 1
    other = partner_swap(value, pairs)
    first = jnp.where(mine == 0, value, other)
    second = jnp.where(mine == 0, other, value)
    return jnp.stack([first, second], axis=axis)


def swap_bit_axes(value, lead, levels):
    order = list(range(value.ndim))
    order[lead : lead + 4] = [lead + 2, lead + 3, lead, lead + 1]
    return jnp.transpose(value, order)


def shards(feats, targets, task_of, counts, down_w, up_w, head):
    groups = lax.axis_size("task")
    peers = lax.axis_size("ex")
    levels = peers.bit_length() - 1
    sources = feats.shape[0]
    side = feats.shape[1]
    chans = feats.shape[3]
    cells = side * side
    bucket = (2 * sources + groups - 1) // groups
    order = jnp.arange(sources, dtype=jnp.int32)
    earlier = (task_of[:, None] == task_of[None, :]) & (order[None, :] < order[:, None])
    position = jnp.sum(earlier.astype(jnp.int32), axis=1)
    send_labels = (
        jnp.full((groups, bucket, cells), -1.0, jnp.bfloat16)
        .at[task_of, position]
        .set(targets.astype(jnp.bfloat16))
    )
    send_feats = (
        jnp.zeros((groups, bucket + 1, side, side, chans), jnp.bfloat16)
        .at[task_of, position]
        .set(feats)
        .at[:, bucket, 0, 0, : bucket * cells]
        .set(send_labels.reshape(groups, bucket * cells))
    )
    come_feats = lax.all_to_all(send_feats, "task", split_axis=0, concat_axis=0, tiled=True)
    held_feats = come_feats[:, :bucket].reshape(groups * bucket, side, side, chans)
    held_labels = come_feats[:, bucket, 0, 0, : bucket * cells]
    held_labels = held_labels.reshape(groups * bucket, cells).astype(jnp.int32)
    count = counts[0].astype(jnp.float32)
    entries = 10.0 * CHANNELS * INNER
    place = lax.axis_index("ex")
    part_chans = down_w.shape[3] // peers
    part_inner = up_w.shape[1] // peers
    inner = down_w.shape[4]
    collected = []
    down_low = down_w[0].astype(jnp.bfloat16)
    upper_low = up_w[0].astype(jnp.bfloat16)
    down_own = lax.dynamic_slice_in_dim(down_w[0], place * part_chans, part_chans, 2)
    up_own = lax.dynamic_slice_in_dim(up_w[0], place * part_inner, part_inner, 0)
    bits_shape = (2,) * levels
    core = place % 2
    second_core = core == 1
    orders = ([0, 1, 2, 3, 4], [0, 3, 4, 1, 2])
    for update_round in range(TRAIN_STEPS):
        loss_sum, grad_down, grad_up = train_pass(
            held_feats, held_labels, down_low, upper_low, head, count
        )
        grad_down = grad_down.reshape((3, 3) + bits_shape + (part_chans, inner))
        grad_up = grad_up.reshape(bits_shape + (part_inner, up_w.shape[2]))
        for stage in range(levels):
            if stage == 1:
                grad_down = jnp.where(second_core, swap_bit_axes(grad_down, 2, levels), grad_down)
                grad_up = jnp.where(second_core, swap_bit_axes(grad_up, 0, levels), grad_up)
            bits_of = (orders[0][stage], orders[1][stage])
            pairs = stage_pairs(bits_of, peers)
            bit = jnp.where(second_core, bits_of[1], bits_of[0])
            grad_down = halve_sum(grad_down, 2 + levels - 1 - stage, bit, pairs, place)
            grad_up = halve_sum(grad_up, levels - 1 - stage, bit, pairs, place)
        squares = jnp.sum(grad_down * grad_down) + jnp.sum(grad_up * grad_up)
        totals = jnp.stack([squares, loss_sum])
        spread = jnp.broadcast_to(totals[None, :], (peers, totals.shape[0]))
        totals = jnp.sum(lax.all_to_all(spread, "ex", 0, 0, tiled=True), axis=0)
        scale = step_scale(totals[0], entries)
        down_own = down_own - scale * grad_down
        up_own = up_own - scale * grad_up
        collected.append(totals[1] / (count * cells))
        if update_round + 1 < TRAIN_STEPS:
            down_low = down_own.astype(jnp.bfloat16)
            upper_low = up_own.astype(jnp.bfloat16)
            for step_index in range(levels):
                stage = levels - 1 - step_index
                if stage == 0:
                    down_low = jnp.where(second_core, swap_bit_axes(down_low, 2, levels), down_low)
                    upper_low = jnp.where(second_core, swap_bit_axes(upper_low, 0, levels), upper_low)
                bits_of = (orders[0][stage], orders[1][stage])
                pairs = stage_pairs(bits_of, peers)
                bit = jnp.where(second_core, bits_of[1], bits_of[0])
                down_low = double_join(down_low, 2 + step_index, bit, pairs, place)
                upper_low = double_join(upper_low, step_index, bit, pairs, place)
            down_low = down_low.reshape(down_w.shape[1:])
            upper_low = upper_low.reshape(up_w.shape[1:])
    return (down_own[None], up_own[None], jnp.stack(collected)[None])


def solution(mesh):
    placed = (
        P(("task", "ex"), None, None, None),
        P(("task", "ex"), None),
        P(("task", "ex")),
        P("task"),
        P("task", None, None, None, None),
        P("task", None, None),
        P(),
    )
    return jax.shard_map(
        shards,
        mesh=mesh,
        in_specs=placed,
        out_specs=(P("task", None, None, "ex", None), P("task", "ex", None), P("task", None)),
        check_vma=False,
    )
```

```python
import jax
import jax.numpy as jnp
from jax import lax
from jax.sharding import PartitionSpec as P

CHANNELS = 512
INNER = 256
TRAIN_STEPS = 2


def shifted_windows(grids):
    count_rows = grids.shape[0]
    side = grids.shape[1]
    padded = jnp.pad(grids, ((0, 0), (1, 1), (1, 1), (0, 0)))
    windows = []
    for offset_index in range(9):
        row_shift = offset_index // 3
        col_shift = offset_index % 3
        window = padded[:, row_shift : row_shift + side, col_shift : col_shift + side, :]
        windows.append(window.reshape(count_rows * side * side, grids.shape[3]))
    return windows


def contract_rows(left, right):
    return lax.dot_general(
        left, right, (((0,), (0,)), ((), ())), preferred_element_type=jnp.float32
    )


def train_pass(grids, labels, down_low, up_low, head, count):
    windows = shifted_windows(grids)
    flat_rows = windows[0].shape[0]
    middle = jnp.zeros((flat_rows, down_low.shape[3]), jnp.float32)
    for offset_index in range(9):
        middle = middle + jnp.dot(
            windows[offset_index],
            down_low[offset_index // 3, offset_index % 3],
            preferred_element_type=jnp.float32,
        )
    active = jax.nn.silu(middle).astype(jnp.bfloat16)
    hidden = grids.reshape(flat_rows, grids.shape[3]).astype(jnp.float32) + jnp.dot(
        active, up_low, preferred_element_type=jnp.float32
    )
    inverse = lax.rsqrt(jnp.mean(hidden * hidden, axis=-1, keepdims=True) + 1e-06)
    normed = hidden * inverse
    head_wide = head.astype(jnp.float32)
    logits = jnp.dot(
        normed, head_wide, precision=lax.Precision.HIGHEST, preferred_element_type=jnp.float32
    )
    flat_labels = labels.reshape(flat_rows)
    living = (flat_labels >= 0).astype(jnp.float32)
    onehot = (flat_labels[:, None] == jnp.arange(head.shape[1], dtype=jnp.int32)[None, :]).astype(
        jnp.float32
    )
    powers = jnp.exp(logits)
    totals = jnp.sum(powers, axis=-1)
    loss_sum = jnp.sum((jnp.log(totals) - jnp.sum(logits * onehot, axis=-1)) * living)
    dlogits = (powers / totals[:, None] - onehot) * living[:, None] / count
    dnormed = lax.dot_general(
        dlogits,
        head_wide,
        (((1,), (1,)), ((), ())),
        precision=lax.Precision.HIGHEST,
        preferred_element_type=jnp.float32,
    )
    dhidden = (
        inverse * (dnormed - normed * jnp.mean(dnormed * normed, axis=-1, keepdims=True))
    ).astype(jnp.bfloat16)
    grad_up = contract_rows(active, dhidden)
    dactive = lax.dot_general(
        dhidden, up_low, (((1,), (1,)), ((), ())), preferred_element_type=jnp.float32
    )
    sigmoid = jax.nn.sigmoid(middle)
    dmiddle = (dactive * sigmoid * (1.0 + middle * (1.0 - sigmoid))).astype(jnp.bfloat16)
    grad_down = jnp.stack([contract_rows(window, dmiddle) for window in windows])
    grad_down = grad_down.reshape(3, 3, grids.shape[3], down_low.shape[3])
    return (loss_sum, grad_down, grad_up)


def step_scale(squares, entries):
    return 0.004 * lax.rsqrt(squares / entries + 1e-06)


def partner_swap(value, pairs):
    return lax.ppermute(value, "ex", perm=pairs)


def stage_pairs(bits_of, peers):
    return [(i, i ^ (1 << bits_of[i % 2])) for i in range(peers)]


def halve_sum(value, axis, bit, pairs, place):
    mine = (place >> bit) & 1
    keep = lax.dynamic_index_in_dim(value, mine, axis, keepdims=False)
    give = lax.dynamic_index_in_dim(value, 1 - mine, axis, keepdims=False)
    sent = partner_swap(give.astype(jnp.bfloat16), pairs)
    return keep + sent.astype(jnp.float32)


def double_join(value, axis, bit, pairs, place):
    mine = (place >> bit) & 1
    other = partner_swap(value, pairs)
    joined = jnp.zeros(value.shape[:axis] + (2,) + value.shape[axis:], value.dtype)
    joined = lax.dynamic_update_slice_in_dim(joined, jnp.expand_dims(value, axis), mine, axis)
    return lax.dynamic_update_slice_in_dim(joined, jnp.expand_dims(other, axis), 1 - mine, axis)


def swap_bit_axes(value, lead, levels):
    order = list(range(value.ndim))
    order[lead : lead + 4] = [lead + 2, lead + 3, lead, lead + 1]
    return jnp.transpose(value, order)


def shards(feats, targets, task_of, counts, down_w, up_w, head):
    groups = lax.axis_size("task")
    peers = lax.axis_size("ex")
    levels = peers.bit_length() - 1
    sources = feats.shape[0]
    side = feats.shape[1]
    chans = feats.shape[3]
    cells = side * side
    bucket = (2 * sources + groups - 1) // groups
    order = jnp.arange(sources, dtype=jnp.int32)
    earlier = (task_of[:, None] == task_of[None, :]) & (order[None, :] < order[:, None])
    position = jnp.sum(earlier.astype(jnp.int32), axis=1)
    send_feats = (
        jnp.zeros((groups, bucket, side, side, chans), jnp.bfloat16)
        .at[task_of, position]
        .set(feats)
    )
    send_labels = (
        jnp.full((groups, bucket, cells), -1.0, jnp.bfloat16)
        .at[task_of, position]
        .set(targets.astype(jnp.bfloat16))
    )
    come_feats, come_labels = (
        lax.all_to_all(send_feats, "task", split_axis=0, concat_axis=0, tiled=True),
        lax.all_to_all(send_labels, "task", split_axis=0, concat_axis=0, tiled=True),
    )
    held_feats = come_feats.reshape(groups * bucket, side, side, chans)
    held_labels = come_labels.reshape(groups * bucket, cells).astype(jnp.int32)
    count = counts[0].astype(jnp.float32)
    entries = 10.0 * CHANNELS * INNER
    place = lax.axis_index("ex")
    part_chans = down_w.shape[3] // peers
    part_inner = up_w.shape[1] // peers
    inner = down_w.shape[4]
    collected = []
    down_low = down_w[0].astype(jnp.bfloat16)
    upper_low = up_w[0].astype(jnp.bfloat16)
    down_own = lax.dynamic_slice_in_dim(down_w[0], place * part_chans, part_chans, 2)
    up_own = lax.dynamic_slice_in_dim(up_w[0], place * part_inner, part_inner, 0)
    bits_shape = (2,) * levels
    core = place % 2
    second_core = core == 1
    orders = ([0, 1, 2, 3, 4], [0, 3, 4, 1, 2])
    for update_round in range(TRAIN_STEPS):
        loss_sum, grad_down, grad_up = train_pass(
            held_feats, held_labels, down_low, upper_low, head, count
        )
        grad_down = grad_down.reshape((3, 3) + bits_shape + (part_chans, inner))
        grad_up = grad_up.reshape(bits_shape + (part_inner, up_w.shape[2]))
        for stage in range(levels):
            if stage == 1:
                grad_down = jnp.where(second_core, swap_bit_axes(grad_down, 2, levels), grad_down)
                grad_up = jnp.where(second_core, swap_bit_axes(grad_up, 0, levels), grad_up)
            bits_of = (orders[0][stage], orders[1][stage])
            pairs = stage_pairs(bits_of, peers)
            bit = jnp.where(second_core, bits_of[1], bits_of[0])
            grad_down = halve_sum(grad_down, 2 + levels - 1 - stage, bit, pairs, place)
            grad_up = halve_sum(grad_up, levels - 1 - stage, bit, pairs, place)
        squares = jnp.sum(grad_down * grad_down) + jnp.sum(grad_up * grad_up)
        totals = jnp.stack([squares, loss_sum])
        spread = jnp.broadcast_to(totals[None, :], (peers, totals.shape[0]))
        totals = jnp.sum(lax.all_to_all(spread, "ex", 0, 0, tiled=True), axis=0)
        scale = step_scale(totals[0], entries)
        down_own = down_own - scale * grad_down
        up_own = up_own - scale * grad_up
        collected.append(totals[1] / (count * cells))
        if update_round + 1 < TRAIN_STEPS:
            down_low = down_own.astype(jnp.bfloat16)
            upper_low = up_own.astype(jnp.bfloat16)
            for step_index in range(levels):
                stage = levels - 1 - step_index
                if stage == 0:
                    down_low = jnp.where(second_core, swap_bit_axes(down_low, 2, levels), down_low)
                    upper_low = jnp.where(second_core, swap_bit_axes(upper_low, 0, levels), upper_low)
                bits_of = (orders[0][stage], orders[1][stage])
                pairs = stage_pairs(bits_of, peers)
                bit = jnp.where(second_core, bits_of[1], bits_of[0])
                down_low = double_join(down_low, 2 + step_index, bit, pairs, place)
                upper_low = double_join(upper_low, step_index, bit, pairs, place)
            down_low = down_low.reshape(down_w.shape[1:])
            upper_low = upper_low.reshape(up_w.shape[1:])
    return (down_own[None], up_own[None], jnp.stack(collected)[None])


def solution(mesh):
    placed = (
        P(("task", "ex"), None, None, None),
        P(("task", "ex"), None),
        P(("task", "ex")),
        P("task"),
        P("task", None, None, None, None),
        P("task", None, None),
        P(),
    )
    return jax.shard_map(
        shards,
        mesh=mesh,
        in_specs=placed,
        out_specs=(P("task", None, None, "ex", None), P("task", "ex", None), P("task", None)),
        check_vma=False,
    )
```

```python
import jax
import jax.numpy as jnp
from jax import lax
from jax.sharding import PartitionSpec as P

CHANNELS = 512
INNER = 256
TRAIN_STEPS = 2


def shifted_windows(grids):
    count_rows = grids.shape[0]
    side = grids.shape[1]
    padded = jnp.pad(grids, ((0, 0), (1, 1), (1, 1), (0, 0)))
    windows = []
    for offset_index in range(9):
        row_shift = offset_index // 3
        col_shift = offset_index % 3
        window = padded[:, row_shift : row_shift + side, col_shift : col_shift + side, :]
        windows.append(window.reshape(count_rows * side * side, grids.shape[3]))
    return windows


def contract_rows(left, right):
    return lax.dot_general(
        left, right, (((0,), (0,)), ((), ())), preferred_element_type=jnp.float32
    )


def train_pass(grids, labels, down_low, up_low, head, count):
    windows = shifted_windows(grids)
    flat_rows = windows[0].shape[0]
    middle = jnp.zeros((flat_rows, down_low.shape[3]), jnp.float32)
    for offset_index in range(9):
        middle = middle + jnp.dot(
            windows[offset_index],
            down_low[offset_index // 3, offset_index % 3],
            preferred_element_type=jnp.float32,
        )
    active = jax.nn.silu(middle).astype(jnp.bfloat16)
    hidden = grids.reshape(flat_rows, grids.shape[3]).astype(jnp.float32) + jnp.dot(
        active, up_low, preferred_element_type=jnp.float32
    )
    inverse = lax.rsqrt(jnp.mean(hidden * hidden, axis=-1, keepdims=True) + 1e-06)
    normed = hidden * inverse
    head_wide = head.astype(jnp.float32)
    logits = jnp.dot(
        normed, head_wide, precision=lax.Precision.HIGHEST, preferred_element_type=jnp.float32
    )
    flat_labels = labels.reshape(flat_rows)
    living = (flat_labels >= 0).astype(jnp.float32)
    onehot = (flat_labels[:, None] == jnp.arange(head.shape[1], dtype=jnp.int32)[None, :]).astype(
        jnp.float32
    )
    powers = jnp.exp(logits)
    totals = jnp.sum(powers, axis=-1)
    loss_sum = jnp.sum((jnp.log(totals) - jnp.sum(logits * onehot, axis=-1)) * living)
    dlogits = (powers / totals[:, None] - onehot) * living[:, None] / count
    dnormed = lax.dot_general(
        dlogits,
        head_wide,
        (((1,), (1,)), ((), ())),
        precision=lax.Precision.HIGHEST,
        preferred_element_type=jnp.float32,
    )
    dhidden = (
        inverse * (dnormed - normed * jnp.mean(dnormed * normed, axis=-1, keepdims=True))
    ).astype(jnp.bfloat16)
    grad_up = contract_rows(active, dhidden)
    dactive = lax.dot_general(
        dhidden, up_low, (((1,), (1,)), ((), ())), preferred_element_type=jnp.float32
    )
    sigmoid = jax.nn.sigmoid(middle)
    dmiddle = (dactive * sigmoid * (1.0 + middle * (1.0 - sigmoid))).astype(jnp.bfloat16)
    grad_down = jnp.stack([contract_rows(window, dmiddle) for window in windows])
    grad_down = grad_down.reshape(3, 3, grids.shape[3], down_low.shape[3])
    return (loss_sum, grad_down, grad_up)


def step_scale(squares, entries):
    return 0.004 * lax.rsqrt(squares / entries + 1e-06)


def partner_swap(value, pairs):
    return lax.ppermute(value, "ex", perm=pairs)


def stage_pairs(bits_of, peers):
    return [(i, i ^ (1 << bits_of[i % 2])) for i in range(peers)]


def halve_sum(value, axis, bit, pairs, place):
    mine = (place >> bit) & 1
    keep = lax.dynamic_index_in_dim(value, mine, axis, keepdims=False)
    give = lax.dynamic_index_in_dim(value, 1 - mine, axis, keepdims=False)
    sent = partner_swap(give.astype(jnp.bfloat16), pairs)
    return keep + sent.astype(jnp.float32)


def double_join(value, axis, bit, pairs, place):
    mine = (place >> bit) & 1
    other = partner_swap(value, pairs)
    first = jnp.where(mine == 0, value, other)
    second = jnp.where(mine == 0, other, value)
    return jnp.stack([first, second], axis=axis)


def swap_bit_axes(value, lead, levels):
    order = list(range(value.ndim))
    order[lead : lead + 4] = [lead + 2, lead + 3, lead, lead + 1]
    return jnp.transpose(value, order)


def shards(feats, targets, task_of, counts, down_w, up_w, head):
    groups = lax.axis_size("task")
    peers = lax.axis_size("ex")
    levels = peers.bit_length() - 1
    sources = feats.shape[0]
    side = feats.shape[1]
    chans = feats.shape[3]
    cells = side * side
    bucket = (2 * sources + groups - 1) // groups
    order = jnp.arange(sources, dtype=jnp.int32)
    earlier = (task_of[:, None] == task_of[None, :]) & (order[None, :] < order[:, None])
    position = jnp.sum(earlier.astype(jnp.int32), axis=1)
    send_feats = (
        jnp.zeros((groups, bucket, side, side, chans), jnp.bfloat16)
        .at[task_of, position]
        .set(feats)
    )
    send_labels = (
        jnp.full((groups, bucket, cells), -1.0, jnp.bfloat16)
        .at[task_of, position]
        .set(targets.astype(jnp.bfloat16))
    )
    come_feats, come_labels = (
        lax.all_to_all(send_feats, "task", split_axis=0, concat_axis=0, tiled=True),
        lax.all_to_all(send_labels, "task", split_axis=0, concat_axis=0, tiled=True),
    )
    held_feats = come_feats.reshape(groups * bucket, side, side, chans)
    held_labels = come_labels.reshape(groups * bucket, cells).astype(jnp.int32)
    count = counts[0].astype(jnp.float32)
    entries = 10.0 * CHANNELS * INNER
    place = lax.axis_index("ex")
    part_chans = down_w.shape[3] // peers
    part_inner = up_w.shape[1] // peers
    inner = down_w.shape[4]
    collected = []
    down_low = down_w[0].astype(jnp.bfloat16)
    upper_low = up_w[0].astype(jnp.bfloat16)
    down_own = lax.dynamic_slice_in_dim(down_w[0], place * part_chans, part_chans, 2)
    up_own = lax.dynamic_slice_in_dim(up_w[0], place * part_inner, part_inner, 0)
    bits_shape = (2,) * levels
    core = place % 2
    second_core = core == 1
    orders = ([0, 1, 2, 3, 4], [0, 3, 4, 1, 2])
    for update_round in range(TRAIN_STEPS):
        loss_sum, grad_down, grad_up = train_pass(
            held_feats, held_labels, down_low, upper_low, head, count
        )
        grad_down = grad_down.reshape((3, 3) + bits_shape + (part_chans, inner))
        grad_up = grad_up.reshape(bits_shape + (part_inner, up_w.shape[2]))
        for stage in range(levels):
            if stage == 1:
                grad_down = jnp.where(second_core, swap_bit_axes(grad_down, 2, levels), grad_down)
                grad_up = jnp.where(second_core, swap_bit_axes(grad_up, 0, levels), grad_up)
            bits_of = (orders[0][stage], orders[1][stage])
            pairs = stage_pairs(bits_of, peers)
            bit = jnp.where(second_core, bits_of[1], bits_of[0])
            grad_down = halve_sum(grad_down, 2 + levels - 1 - stage, bit, pairs, place)
            grad_up = halve_sum(grad_up, levels - 1 - stage, bit, pairs, place)
        squares = jnp.sum(grad_down * grad_down) + jnp.sum(grad_up * grad_up)
        totals = jnp.stack([squares, loss_sum])
        spread = jnp.broadcast_to(totals[None, :], (peers, totals.shape[0]))
        totals = jnp.sum(lax.all_to_all(spread, "ex", 0, 0, tiled=True), axis=0)
        scale = step_scale(totals[0], entries)
        down_own = down_own - scale * grad_down
        up_own = up_own - scale * grad_up
        collected.append(totals[1] / (count * cells))
        if update_round + 1 < TRAIN_STEPS:
            down_low = down_own.astype(jnp.bfloat16)
            upper_low = up_own.astype(jnp.bfloat16)
            for step_index in range(levels):
                stage = levels - 1 - step_index
                bits_of = (orders[0][stage], orders[0][stage])
                pairs = stage_pairs(bits_of, peers)
                bit = jnp.where(second_core, bits_of[1], bits_of[0])
                down_low = double_join(down_low, 2 + step_index, bit, pairs, place)
                upper_low = double_join(upper_low, step_index, bit, pairs, place)
            down_low = down_low.reshape(down_w.shape[1:])
            upper_low = upper_low.reshape(up_w.shape[1:])
    return (down_own[None], up_own[None], jnp.stack(collected)[None])


def solution(mesh):
    placed = (
        P(("task", "ex"), None, None, None),
        P(("task", "ex"), None),
        P(("task", "ex")),
        P("task"),
        P("task", None, None, None, None),
        P("task", None, None),
        P(),
    )
    return jax.shard_map(
        shards,
        mesh=mesh,
        in_specs=placed,
        out_specs=(P("task", None, None, "ex", None), P("task", "ex", None), P("task", None)),
        check_vma=False,
    )
```
